256 devices in a mesh: expert: 64 (over x, z, core), tensor: 4 (over y).
Axes of the slice: x: 4, y: 4, z: 8, core: 2. Of those that a mesh axis runs over, the one named last changes fastest.
Arguments:
- tokens: bfloat16 [8192, 3584], P('expert'), may hold values from -6 to 6
- cotangent: bfloat16 [8192, 3584], P('expert'), may hold values from -6 to 6
- chosen_experts: int32 [8192, 8], P('expert'), may hold values from 0 to 255, as said below
- chosen_slots: int32 [8192, 8], P('expert'), may hold values from 0 to 127, as said below
- routing_gate_weight: float32 [8192, 8], P('expert'), may hold values from 0.1 to 1
- padded_slot_count: int32 [64, 64], P('expert'), may hold values from 0 to 8, as said below
- w_gate: bfloat16 [64, 3584, 1024], P('expert', None, 'tensor'), may hold values from -0.09375 to 0.09375
- w_up: bfloat16 [64, 3584, 1024], P('expert', None, 'tensor'), may hold values from -0.09375 to 0.09375
- w_down: bfloat16 [64, 1024, 3584], P('expert', 'tensor'), may hold values from -0.1875 to 0.1875
Outputs:
- mixed: bfloat16 [8192, 3584], P('expert', 'tensor')
- token_gradient: bfloat16 [8192, 3584], P('expert', 'tensor')
- gate_gradient: float32 [8192, 8], P('expert')
- grad_w_gate: bfloat16 [64, 3584, 1024], P('expert', None, 'tensor')
- grad_w_up: bfloat16 [64, 3584, 1024], P('expert', None, 'tensor')
- grad_w_down: bfloat16 [64, 1024, 3584], P('expert', 'tensor')
The draws below stay inside these ranges and needn't reach their ends.
Inputs may be any that keep to these rules, and one draw needn't show every extreme that they name: `chosen_experts`: each token names 8 different experts; only experts under 64 are in flight. `chosen_slots`: within one block of 128 tokens, the routes that name one expert are numbered 0, 1, 2 and so on in order of token and then of route. In every block some expert in flight is named by every token. padded_slot_count[s, e] is the smaller of 8 and the number of routes of block s that name expert e; in every block some expert reaches 8, and some expert in flight is named by no route.
All inputs are finite; a program needn't handle non-finite values.
Results may differ from the reference program's by a relative error of at most 0.015.
Values may be sent and summed in bfloat16 or wider, within the bound.
No kernel may reach another device: no remote copies, remote signals or barrier semaphores. Data moves between devices by JAX's collectives and lax.ppermute only.
A program may use at most 128 MiB of HBM per device.

```python
import math
import jax
import jax.numpy as jnp
from jax import lax

D = 3584
HID = 1024
TOP = 8
TOK_DEV = 128
SOURCES = 64
EXPERTS = 64
ROUTED = 256
TOKENS = 8192
SLOT_CAPACITY = 8
N_TENSOR = 4


def routing_tables(key):
    noise = jax.random.randint(jax.random.fold_in(key, 101), (TOKENS, ROUTED), 0, 4096)
    favour = jax.random.randint(jax.random.fold_in(key, 102), (ROUTED,), 0, 512)
    hottest = jax.random.randint(jax.random.fold_in(key, 103), (), 0, EXPERTS)
    columns = jnp.arange(ROUTED, dtype=jnp.int32)
    unnamed = jnp.where(hottest < EXPERTS - 1, hottest + 1, 1)
    base = (noise + favour[None, :]) * ROUTED + columns[None, :]
    base = jnp.where(columns[None, :] == unnamed, columns[None, :], base)
    score = jnp.where(columns[None, :] == hottest, (noise + 16384) * ROUTED + columns[None, :], base)
    chosen = lax.top_k(score.astype(jnp.int32), TOP)[1].astype(jnp.int32)
    one_hot = (chosen[:, :, None] == columns[None, None, :]).astype(jnp.int32)
    flat = one_hot.reshape(SOURCES, TOK_DEV * TOP, ROUTED)
    before = jnp.cumsum(flat, axis=1) - flat
    slots = jnp.sum(before * flat, axis=2).reshape(TOKENS, TOP).astype(jnp.int32)
    counts = jnp.minimum(jnp.sum(flat, axis=1), SLOT_CAPACITY)[:, :EXPERTS].astype(jnp.int32)
    return (chosen, slots, counts)


def draw_chosen_experts(key, part):
    return routing_tables(key)[0]


def draw_chosen_slots(key, part):
    return routing_tables(key)[1]


def draw_padded_slot_count(key, part):
    return routing_tables(key)[2]


def levels(own_key, dims, cuts, least, top_value):
    level = 1.0
    for axis_at, parts in cuts:
        steps = jax.random.uniform(jax.random.fold_in(jax.random.fold_in(own_key, 6), axis_at), (parts,), jnp.float32, least / len(cuts), top_value / len(cuts))
        level = level * jnp.repeat(jnp.exp(steps), dims[axis_at] // parts).reshape((-1,) + (1,) * (len(dims) - 1 - axis_at))
    return level


def centred(rng, shape, spread, limit, cuts=(), held_as=jnp.bfloat16):
    level = levels(rng, shape, cuts, -0.22, 0.18) if cuts else 1.0
    drawn = jax.random.normal(rng, shape, jnp.float32) * spread * level
    return jnp.minimum(jnp.maximum(drawn, -limit), limit).astype(held_as)


def setup_inputs(seed: int = 0) -> dict:
    splits = jax.random.split(jax.random.key(seed), 10)
    return {
        "tokens": centred(splits[0], (TOKENS, D), 1.0, 6.0, ((0, 64),)),
        "cotangent": centred(splits[1], (TOKENS, D), 1.0, 6.0, ((0, 64),)),
        "chosen_experts": draw_chosen_experts(jax.random.fold_in(splits[9], 71), 0),
        "chosen_slots": draw_chosen_slots(jax.random.fold_in(splits[9], 71), 0),
        "routing_gate_weight": jnp.clip(jnp.exp(math.log(1.0) - 2.3025851 * jax.random.uniform(splits[4], (TOKENS, TOP), jnp.float32) ** levels(splits[4], (TOKENS, TOP), ((0, 64),), -0.2, 0.2)), 0.1, 1.0),
        "padded_slot_count": draw_padded_slot_count(jax.random.fold_in(splits[9], 71), 0),
        "w_gate": centred(splits[6], (EXPERTS, D, HID), D ** -0.5, 0.09375, ((0, 64), (2, 4))),
        "w_up": centred(splits[7], (EXPERTS, D, HID), D ** -0.5, 0.09375, ((0, 64), (2, 4))),
        "w_down": centred(splits[8], (EXPERTS, HID, D), HID ** -0.5, 0.1875, ((0, 64), (1, 4))),
    }


def routing_layout(chosen_expert, chosen_slot, slot_count_row, expert_capacity):
    expert_number = slot_count_row.shape[0]
    one_hot = (chosen_expert[:, :, None] == jnp.arange(expert_number, dtype=jnp.int32)[None, None, :]).astype(jnp.int32)
    slot_ceiling = jnp.sum(one_hot * slot_count_row[None, None, :], axis=2)
    slot_alive_mask = (chosen_expert < expert_number) & (chosen_slot < slot_ceiling)
    destination_slot = jnp.where(slot_alive_mask, chosen_expert * expert_capacity + chosen_slot, -1)
    return slot_alive_mask, destination_slot


def pack_slots(tok_block, cot_block, block_gates, destination_slot, send_rows):
    select = destination_slot[None, :, :] == jnp.arange(send_rows, dtype=jnp.int32)[:, None, None]
    picked = jnp.sum(select.astype(jnp.int32), axis=2).astype(jnp.bfloat16)
    slot_gate = jnp.sum(jnp.where(select, block_gates[None, :, :], 0.0), axis=(1, 2))
    token_sum = jnp.dot(picked, tok_block, preferred_element_type=jnp.float32).astype(jnp.bfloat16)
    cot_sum = jnp.dot(picked, cot_block, preferred_element_type=jnp.float32)
    return token_sum, (slot_gate[:, None] * cot_sum).astype(jnp.bfloat16)


def expert_group(expert_rows, expert_cots, gate_weight, up_weight, down_weight):
    pre_gate = jnp.dot(expert_rows, gate_weight, preferred_element_type=jnp.float32)
    pre_up = jnp.dot(expert_rows, up_weight, preferred_element_type=jnp.float32)
    logistic = jax.nn.sigmoid(pre_gate)
    active = pre_gate * logistic
    hidden = (active * pre_up).astype(jnp.bfloat16)
    part_out = jnp.dot(hidden, down_weight, preferred_element_type=jnp.float32)
    grad_hidden = jnp.dot(expert_cots, down_weight.T, preferred_element_type=jnp.float32)
    grad_pre_gate = (grad_hidden * pre_up * logistic * (1.0 + pre_gate * (1.0 - logistic))).astype(jnp.bfloat16)
    grad_pre_up = (grad_hidden * active).astype(jnp.bfloat16)
    part_back = jnp.dot(grad_pre_gate, gate_weight.T, preferred_element_type=jnp.float32) + jnp.dot(grad_pre_up, up_weight.T, preferred_element_type=jnp.float32)
    grad_gate_w = jnp.dot(expert_rows.T, grad_pre_gate, preferred_element_type=jnp.float32).astype(jnp.bfloat16)
    grad_up_w = jnp.dot(expert_rows.T, grad_pre_up, preferred_element_type=jnp.float32).astype(jnp.bfloat16)
    grad_down_w = jnp.dot(hidden.T, expert_cots, preferred_element_type=jnp.float32).astype(jnp.bfloat16)
    return part_out, part_back, (grad_gate_w, grad_up_w, grad_down_w)


def reference(tokens, cotangent, chosen_experts, chosen_slots, routing_gate_weight, padded_slot_count, w_gate, w_up, w_down):
    send_rows = EXPERTS * SLOT_CAPACITY
    group_size = HID // N_TENSOR
    expert_total = SOURCES * SLOT_CAPACITY
    id_blocks = chosen_experts.reshape(SOURCES, TOK_DEV, TOP)
    slot_blocks = chosen_slots.reshape(SOURCES, TOK_DEV, TOP)
    gate_blocks = routing_gate_weight.reshape(SOURCES, TOK_DEV, TOP)
    tok_blocks = tokens.reshape(SOURCES, TOK_DEV, D)
    cot_blocks = cotangent.reshape(SOURCES, TOK_DEV, D)

    def pack_source(record):
        chosen_expert, chosen_slot, block_gates, slot_count_row, tok_block, cot_block = record
        slot_alive_mask, destination_slot = routing_layout(chosen_expert, chosen_slot, slot_count_row, SLOT_CAPACITY)
        return pack_slots(tok_block, cot_block, block_gates, destination_slot, send_rows)

    token_buf, cot_buf = lax.map(pack_source, (id_blocks, slot_blocks, gate_blocks, padded_slot_count, tok_blocks, cot_blocks))
    rows_all = token_buf.reshape(SOURCES, EXPERTS, SLOT_CAPACITY, D).transpose(1, 0, 2, 3).reshape(EXPERTS, expert_total, D)
    cots_all = cot_buf.reshape(SOURCES, EXPERTS, SLOT_CAPACITY, D).transpose(1, 0, 2, 3).reshape(EXPERTS, expert_total, D)

    def run_expert(record):
        expert_rows, expert_cots, gate_weight, up_weight, down_weight = record
        total_out = jnp.zeros((expert_total, D), jnp.float32)
        total_back = jnp.zeros((expert_total, D), jnp.float32)
        gate_list, up_list, down_list = [], [], []
        for shard in range(N_TENSOR):
            first = shard * group_size
            part_out, part_back, grads = expert_group(expert_rows, expert_cots, gate_weight[:, first:first + group_size], up_weight[:, first:first + group_size], down_weight[first:first + group_size, :])
            total_out = total_out + lax.optimization_barrier(part_out.astype(jnp.bfloat16)).astype(jnp.float32)
            total_back = total_back + lax.optimization_barrier(part_back.astype(jnp.bfloat16)).astype(jnp.float32)
            gate_list.append(grads[0])
            up_list.append(grads[1])
            down_list.append(grads[2])
        return (total_out.astype(jnp.bfloat16), total_back.astype(jnp.bfloat16), jnp.concatenate(gate_list, axis=1), jnp.concatenate(up_list, axis=1), jnp.concatenate(down_list, axis=0))

    expert_out, expert_back, grad_w_gate, grad_w_up, grad_w_down = lax.map(run_expert, (rows_all, cots_all, w_gate, w_up, w_down))
    back_out = expert_out.reshape(EXPERTS, SOURCES, SLOT_CAPACITY, D).transpose(1, 0, 2, 3).reshape(SOURCES, send_rows, D)
    back_grad = expert_back.reshape(EXPERTS, SOURCES, SLOT_CAPACITY, D).transpose(1, 0, 2, 3).reshape(SOURCES, send_rows, D)

    def combine_rows(record):
        chosen_expert, chosen_slot, block_gates, slot_count_row, cot_block, slot_out, slot_back = record
        slot_alive_mask, destination_slot = routing_layout(chosen_expert, chosen_slot, slot_count_row, SLOT_CAPACITY)
        positions = jnp.maximum(destination_slot, 0).reshape(-1)
        out_rows = jnp.take(slot_out, positions, axis=0).reshape(TOK_DEV, TOP, D).astype(jnp.float32)
        returned_rows = jnp.take(slot_back, positions, axis=0).reshape(TOK_DEV, TOP, D).astype(jnp.float32)
        gate_scaling = jnp.where(slot_alive_mask, block_gates, 0.0)
        mixed = jnp.sum(gate_scaling[:, :, None] * out_rows, axis=1).astype(jnp.bfloat16)
        token_gradient_rows = jnp.sum(jnp.where(slot_alive_mask[:, :, None], returned_rows, 0.0), axis=1).astype(jnp.bfloat16)
        hidden_totals = jnp.sum(cot_block.astype(jnp.float32)[:, None, :] * out_rows, axis=2)
        return mixed, token_gradient_rows, jnp.where(slot_alive_mask, hidden_totals, 0.0)

    mixed, token_gradient, gate_gradient = lax.map(combine_rows, (id_blocks, slot_blocks, gate_blocks, padded_slot_count, cot_blocks, back_out, back_grad))
    return (mixed.reshape(TOKENS, D), token_gradient.reshape(TOKENS, D), gate_gradient.reshape(TOKENS, TOP), grad_w_gate, grad_w_up, grad_w_down)
```

```python
import jax
import jax.numpy as jnp
from jax import lax
from jax.sharding import PartitionSpec as P

OWNED = 4


def routing_layout(chosen_expert, chosen_slot, slot_count_row, expert_capacity):
    expert_number = slot_count_row.shape[0]
    one_hot = (
        chosen_expert[:, :, None] == jnp.arange(expert_number, dtype=jnp.int32)[None, None, :]
    ).astype(jnp.int32)
    slot_ceiling = jnp.sum(one_hot * slot_count_row[None, None, :], axis=2)
    slot_alive_mask = (chosen_expert < expert_number) & (chosen_slot < slot_ceiling)
    destination_slot = jnp.where(slot_alive_mask, chosen_expert * expert_capacity + chosen_slot, -1)
    return (slot_alive_mask, destination_slot)


def pack_slots(tok_block, cot_block, block_gates, destination_slot, send_rows):
    select = destination_slot[None, :, :] == jnp.arange(send_rows, dtype=jnp.int32)[:, None, None]
    picked = jnp.sum(select.astype(jnp.int32), axis=2).astype(jnp.bfloat16)
    slot_gate = jnp.sum(jnp.where(select, block_gates[None, :, :], 0.0), axis=(1, 2))
    token_sum = jnp.dot(picked, tok_block, preferred_element_type=jnp.float32).astype(jnp.bfloat16)
    cot_sum = jnp.dot(picked, cot_block, preferred_element_type=jnp.float32)
    return (token_sum, (slot_gate[:, None] * cot_sum).astype(jnp.bfloat16))


def expert_group(expert_rows, expert_cots, gate_weight, up_weight, down_weight):
    pre_gate = jnp.dot(expert_rows, gate_weight, preferred_element_type=jnp.float32)
    pre_up = jnp.dot(expert_rows, up_weight, preferred_element_type=jnp.float32)
    logistic = jax.nn.sigmoid(pre_gate)
    active = pre_gate * logistic
    hidden = (active * pre_up).astype(jnp.bfloat16)
    part_out = jnp.dot(hidden, down_weight, preferred_element_type=jnp.float32)
    grad_hidden = jnp.dot(expert_cots, down_weight.T, preferred_element_type=jnp.float32)
    grad_pre_gate = (grad_hidden * pre_up * logistic * (1.0 + pre_gate * (1.0 - logistic))).astype(
        jnp.bfloat16
    )
    grad_pre_up = (grad_hidden * active).astype(jnp.bfloat16)
    part_back = jnp.dot(grad_pre_gate, gate_weight.T, preferred_element_type=jnp.float32) + jnp.dot(
        grad_pre_up, up_weight.T, preferred_element_type=jnp.float32
    )
    grad_gate_w = jnp.dot(expert_rows.T, grad_pre_gate, preferred_element_type=jnp.float32).astype(
        jnp.bfloat16
    )
    grad_up_w = jnp.dot(expert_rows.T, grad_pre_up, preferred_element_type=jnp.float32).astype(
        jnp.bfloat16
    )
    grad_down_w = jnp.dot(hidden.T, expert_cots, preferred_element_type=jnp.float32).astype(
        jnp.bfloat16
    )
    return (part_out, part_back, (grad_gate_w, grad_up_w, grad_down_w))


def expert_group_t(expert_rows, expert_cots, gate_weight, up_weight, down_weight):
    pre_gate = jnp.dot(expert_rows, gate_weight, preferred_element_type=jnp.float32)
    pre_up = jnp.dot(expert_rows, up_weight, preferred_element_type=jnp.float32)
    logistic = jax.nn.sigmoid(pre_gate)
    active = pre_gate * logistic
    hidden = (active * pre_up).astype(jnp.bfloat16)
    contract_h = (((1,), (1,)), ((), ()))
    out_t = lax.dot_general(
        down_weight.T, hidden, contract_h, preferred_element_type=jnp.float32
    ).astype(jnp.bfloat16)
    grad_hidden = jnp.dot(expert_cots, down_weight.T, preferred_element_type=jnp.float32)
    grad_pre_gate = (grad_hidden * pre_up * logistic * (1.0 + pre_gate * (1.0 - logistic))).astype(
        jnp.bfloat16
    )
    grad_pre_up = (grad_hidden * active).astype(jnp.bfloat16)
    back_t = (
        lax.dot_general(gate_weight, grad_pre_gate, contract_h, preferred_element_type=jnp.float32)
        + lax.dot_general(up_weight, grad_pre_up, contract_h, preferred_element_type=jnp.float32)
    ).astype(jnp.bfloat16)
    grad_gate_w = jnp.dot(expert_rows.T, grad_pre_gate, preferred_element_type=jnp.float32).astype(
        jnp.bfloat16
    )
    grad_up_w = jnp.dot(expert_rows.T, grad_pre_up, preferred_element_type=jnp.float32).astype(
        jnp.bfloat16
    )
    grad_down_w = jnp.dot(hidden.T, expert_cots, preferred_element_type=jnp.float32).astype(
        jnp.bfloat16
    )
    return (out_t, back_t, (grad_gate_w, grad_up_w, grad_down_w))


def local(
    tokens,
    cotangent,
    chosen_experts,
    chosen_slots,
    routing_gate_weight,
    padded_slot_count,
    w_gate,
    w_up,
    w_down,
):
    tok_rows, feature_width = tokens.shape
    per_token = chosen_experts.shape[1]
    expert_number = padded_slot_count.shape[1]
    expert_capacity = 2 * tok_rows * per_token // (OWNED * lax.axis_size("expert"))
    send_rows = expert_number * expert_capacity
    feature_share = feature_width // lax.axis_size("tensor")
    first_col = lax.axis_index("tensor") * feature_share
    slot_alive_mask, destination_slot = routing_layout(
        chosen_experts, chosen_slots, padded_slot_count[0], expert_capacity
    )
    local_tokens = lax.dynamic_slice_in_dim(tokens, first_col, feature_share, 1)
    local_cotangent_bf = lax.dynamic_slice_in_dim(cotangent, first_col, feature_share, 1)
    token_sum, cot_rows = pack_slots(
        local_tokens, local_cotangent_bf, routing_gate_weight, destination_slot, send_rows
    )
    packed = jnp.stack([token_sum, cot_rows]).reshape(
        2, expert_number, expert_capacity, feature_share
    )
    arrived = lax.all_to_all(packed, "expert", split_axis=1, concat_axis=1, tiled=True)
    arrived = arrived.reshape(2, send_rows, feature_share)
    gathered = lax.all_gather(arrived, "tensor", axis=2, tiled=True)
    expert_rows = gathered[0]
    expert_cots = gathered[1]
    out_t, back_t, grads = expert_group_t(
        expert_rows, expert_cots, w_gate[0], w_up[0], w_down[0]
    )
    total_out = lax.psum_scatter(out_t, "tensor", scatter_dimension=0, tiled=True)
    total_back = lax.psum_scatter(back_t, "tensor", scatter_dimension=0, tiled=True)
    sources = total_out.shape[1] // expert_capacity
    slot_both = jnp.stack([total_out.T, total_back.T]).reshape(
        2, sources, expert_capacity, feature_share
    )
    came = lax.all_to_all(slot_both, "expert", split_axis=1, concat_axis=1, tiled=True)
    came = came.reshape(2, send_rows, feature_share)
    came_out = came[0]
    came_back = came[1]
    positions = jnp.maximum(destination_slot, 0).reshape(-1)
    out_rows = (
        jnp.take(came_out, positions, axis=0)
        .reshape(tok_rows, per_token, feature_share)
        .astype(jnp.float32)
    )
    returned_rows = (
        jnp.take(came_back, positions, axis=0)
        .reshape(tok_rows, per_token, feature_share)
        .astype(jnp.float32)
    )
    gate_scaling = jnp.where(slot_alive_mask, routing_gate_weight, 0.0)
    mixed = jnp.sum(gate_scaling[:, :, None] * out_rows, axis=1).astype(jnp.bfloat16)
    token_gradient = jnp.sum(
        jnp.where(slot_alive_mask[:, :, None], returned_rows, 0.0), axis=1
    ).astype(jnp.bfloat16)
    local_cotangent = local_cotangent_bf.astype(jnp.float32)
    hidden_totals = jnp.sum(local_cotangent[:, None, :] * out_rows, axis=2)
    gate_gradient = lax.psum(jnp.where(slot_alive_mask, hidden_totals, 0.0), "tensor")
    grad_gate_w, grad_up_w, grad_down_w = grads
    return (
        mixed,
        token_gradient,
        gate_gradient,
        grad_gate_w[None],
        grad_up_w[None],
        grad_down_w[None],
    )


def solution(mesh):
    in_specs = (
        P("expert", None),
        P("expert", None),
        P("expert", None),
        P("expert", None),
        P("expert", None),
        P("expert", None),
        P("expert", None, "tensor"),
        P("expert", None, "tensor"),
        P("expert", "tensor", None),
    )
    out_specs = (
        P("expert", "tensor"),
        P("expert", "tensor"),
        P("expert", None),
        P("expert", None, "tensor"),
        P("expert", None, "tensor"),
        P("expert", "tensor", None),
    )
    return jax.shard_map(local, mesh=mesh, in_specs=in_specs, out_specs=out_specs, check_vma=False)
```

```python
import jax
import jax.numpy as jnp
from jax import lax
from jax.sharding import PartitionSpec as P

OWNED = 4


def routing_layout(chosen_expert, chosen_slot, slot_count_row, expert_capacity):
    expert_number = slot_count_row.shape[0]
    one_hot = (
        chosen_expert[:, :, None] == jnp.arange(expert_number, dtype=jnp.int32)[None, None, :]
    ).astype(jnp.int32)
    slot_ceiling = jnp.sum(one_hot * slot_count_row[None, None, :], axis=2)
    slot_alive_mask = (chosen_expert < expert_number) & (chosen_slot < slot_ceiling)
    destination_slot = jnp.where(slot_alive_mask, chosen_expert * expert_capacity + chosen_slot, -1)
    return (slot_alive_mask, destination_slot)


def pack_slots(tok_block, cot_block, block_gates, destination_slot, send_rows):
    select = destination_slot[None, :, :] == jnp.arange(send_rows, dtype=jnp.int32)[:, None, None]
    picked = jnp.sum(select.astype(jnp.int32), axis=2).astype(jnp.bfloat16)
    slot_gate = jnp.sum(jnp.where(select, block_gates[None, :, :], 0.0), axis=(1, 2))
    token_sum = jnp.dot(picked, tok_block, preferred_element_type=jnp.float32).astype(jnp.bfloat16)
    cot_sum = jnp.dot(picked, cot_block, preferred_element_type=jnp.float32)
    return (token_sum, (slot_gate[:, None] * cot_sum).astype(jnp.bfloat16))


def expert_group(expert_rows, expert_cots, gate_weight, up_weight, down_weight):
    pre_gate = jnp.dot(expert_rows, gate_weight, preferred_element_type=jnp.float32)
    pre_up = jnp.dot(expert_rows, up_weight, preferred_element_type=jnp.float32)
    logistic = jax.nn.sigmoid(pre_gate)
    active = pre_gate * logistic
    hidden = (active * pre_up).astype(jnp.bfloat16)
    part_out = jnp.dot(hidden, down_weight, preferred_element_type=jnp.float32)
    grad_hidden = jnp.dot(expert_cots, down_weight.T, preferred_element_type=jnp.float32)
    grad_pre_gate = (grad_hidden * pre_up * logistic * (1.0 + pre_gate * (1.0 - logistic))).astype(
        jnp.bfloat16
    )
    grad_pre_up = (grad_hidden * active).astype(jnp.bfloat16)
    part_back = jnp.dot(grad_pre_gate, gate_weight.T, preferred_element_type=jnp.float32) + jnp.dot(
        grad_pre_up, up_weight.T, preferred_element_type=jnp.float32
    )
    grad_gate_w = jnp.dot(expert_rows.T, grad_pre_gate, preferred_element_type=jnp.float32).astype(
        jnp.bfloat16
    )
    grad_up_w = jnp.dot(expert_rows.T, grad_pre_up, preferred_element_type=jnp.float32).astype(
        jnp.bfloat16
    )
    grad_down_w = jnp.dot(hidden.T, expert_cots, preferred_element_type=jnp.float32).astype(
        jnp.bfloat16
    )
    return (part_out, part_back, (grad_gate_w, grad_up_w, grad_down_w))


def expert_group_t(expert_rows, expert_cots, gate_weight, up_weight, down_weight):
    pre_gate = jnp.dot(expert_rows, gate_weight, preferred_element_type=jnp.float32)
    pre_up = jnp.dot(expert_rows, up_weight, preferred_element_type=jnp.float32)
    logistic = jax.nn.sigmoid(pre_gate)
    active = pre_gate * logistic
    hidden = (active * pre_up).astype(jnp.bfloat16)
    contract_h = (((1,), (1,)), ((), ()))
    out_t = lax.dot_general(
        down_weight.T, hidden, contract_h, preferred_element_type=jnp.float32
    ).astype(jnp.bfloat16)
    grad_hidden = jnp.dot(expert_cots, down_weight.T, preferred_element_type=jnp.float32)
    grad_pre_gate = (grad_hidden * pre_up * logistic * (1.0 + pre_gate * (1.0 - logistic))).astype(
        jnp.bfloat16
    )
    grad_pre_up = (grad_hidden * active).astype(jnp.bfloat16)
    back_t = (
        lax.dot_general(gate_weight, grad_pre_gate, contract_h, preferred_element_type=jnp.float32)
        + lax.dot_general(up_weight, grad_pre_up, contract_h, preferred_element_type=jnp.float32)
    ).astype(jnp.bfloat16)
    grad_gate_w = jnp.dot(expert_rows.T, grad_pre_gate, preferred_element_type=jnp.float32).astype(
        jnp.bfloat16
    )
    grad_up_w = jnp.dot(expert_rows.T, grad_pre_up, preferred_element_type=jnp.float32).astype(
        jnp.bfloat16
    )
    grad_down_w = jnp.dot(hidden.T, expert_cots, preferred_element_type=jnp.float32).astype(
        jnp.bfloat16
    )
    return (out_t, back_t, (grad_gate_w, grad_up_w, grad_down_w))


def local(
    tokens,
    cotangent,
    chosen_experts,
    chosen_slots,
    routing_gate_weight,
    padded_slot_count,
    w_gate,
    w_up,
    w_down,
):
    tok_rows, feature_width = tokens.shape
    per_token = chosen_experts.shape[1]
    expert_number = padded_slot_count.shape[1]
    expert_capacity = 2 * tok_rows * per_token // (OWNED * lax.axis_size("expert"))
    send_rows = expert_number * expert_capacity
    feature_share = feature_width // lax.axis_size("tensor")
    first_col = lax.axis_index("tensor") * feature_share
    slot_alive_mask, destination_slot = routing_layout(
        chosen_experts, chosen_slots, padded_slot_count[0], expert_capacity
    )
    local_tokens = lax.dynamic_slice_in_dim(tokens, first_col, feature_share, 1)
    local_cotangent_bf = lax.dynamic_slice_in_dim(cotangent, first_col, feature_share, 1)
    token_sum, cot_rows = pack_slots(
        local_tokens, local_cotangent_bf, routing_gate_weight, destination_slot, send_rows
    )
    rows_q = lax.all_to_all(
        token_sum.reshape(expert_number, expert_capacity, feature_share),
        "expert", split_axis=0, concat_axis=0, tiled=True,
    ).reshape(send_rows, feature_share)
    rows_all = lax.all_gather(rows_q, "tensor", axis=1, tiled=True)
    cots_q = lax.all_to_all(
        cot_rows.reshape(expert_number, expert_capacity, feature_share),
        "expert", split_axis=0, concat_axis=0, tiled=True,
    ).reshape(send_rows, feature_share)
    cots_all = lax.all_gather(cots_q, "tensor", axis=1, tiled=True)
    out_t, back_t, grads = expert_group_t(
        rows_all, cots_all, w_gate[0], w_up[0], w_down[0]
    )
    total_out = lax.psum_scatter(out_t, "tensor", scatter_dimension=0, tiled=True)
    sources = total_out.shape[1] // expert_capacity
    came_out = lax.all_to_all(
        total_out.T.reshape(sources, expert_capacity, feature_share),
        "expert", split_axis=0, concat_axis=0, tiled=True,
    ).reshape(send_rows, feature_share)
    total_back = lax.psum_scatter(back_t, "tensor", scatter_dimension=0, tiled=True)
    came_back = lax.all_to_all(
        total_back.T.reshape(sources, expert_capacity, feature_share),
        "expert", split_axis=0, concat_axis=0, tiled=True,
    ).reshape(send_rows, feature_share)
    positions = jnp.maximum(destination_slot, 0).reshape(-1)
    out_rows = (
        jnp.take(came_out, positions, axis=0)
        .reshape(tok_rows, per_token, feature_share)
        .astype(jnp.float32)
    )
    returned_rows = (
        jnp.take(came_back, positions, axis=0)
        .reshape(tok_rows, per_token, feature_share)
        .astype(jnp.float32)
    )
    gate_scaling = jnp.where(slot_alive_mask, routing_gate_weight, 0.0)
    mixed = jnp.sum(gate_scaling[:, :, None] * out_rows, axis=1).astype(jnp.bfloat16)
    token_gradient = jnp.sum(
        jnp.where(slot_alive_mask[:, :, None], returned_rows, 0.0), axis=1
    ).astype(jnp.bfloat16)
    local_cotangent = local_cotangent_bf.astype(jnp.float32)
    hidden_totals = jnp.sum(local_cotangent[:, None, :] * out_rows, axis=2)
    gate_gradient = lax.psum(jnp.where(slot_alive_mask, hidden_totals, 0.0), "tensor")
    grad_gate_w, grad_up_w, grad_down_w = grads
    return (
        mixed,
        token_gradient,
        gate_gradient,
        grad_gate_w[None],
        grad_up_w[None],
        grad_down_w[None],
    )


def solution(mesh):
    in_specs = (
        P("expert", None),
        P("expert", None),
        P("expert", None),
        P("expert", None),
        P("expert", None),
        P("expert", None),
        P("expert", None, "tensor"),
        P("expert", None, "tensor"),
        P("expert", "tensor", None),
    )
    out_specs = (
        P("expert", "tensor"),
        P("expert", "tensor"),
        P("expert", None),
        P("expert", None, "tensor"),
        P("expert", None, "tensor"),
        P("expert", "tensor", None),
    )
    return jax.shard_map(local, mesh=mesh, in_specs=in_specs, out_specs=out_specs, check_vma=False)
```

```python
import jax
import jax.numpy as jnp
from jax import lax
from jax.sharding import PartitionSpec as P

OWNED = 4


def routing_layout(chosen_expert, chosen_slot, slot_count_row, expert_capacity):
    expert_number = slot_count_row.shape[0]
    one_hot = (
        chosen_expert[:, :, None] == jnp.arange(expert_number, dtype=jnp.int32)[None, None, :]
    ).astype(jnp.int32)
    slot_ceiling = jnp.sum(one_hot * slot_count_row[None, None, :], axis=2)
    slot_alive_mask = (chosen_expert < expert_number) & (chosen_slot < slot_ceiling)
    destination_slot = jnp.where(slot_alive_mask, chosen_expert * expert_capacity + chosen_slot, -1)
    return (slot_alive_mask, destination_slot)


def pack_slots(tok_block, cot_block, block_gates, destination_slot, send_rows):
    select = destination_slot[None, :, :] == jnp.arange(send_rows, dtype=jnp.int32)[:, None, None]
    picked = jnp.sum(select.astype(jnp.int32), axis=2).astype(jnp.bfloat16)
    slot_gate = jnp.sum(jnp.where(select, block_gates[None, :, :], 0.0), axis=(1, 2))
    token_sum = jnp.dot(picked, tok_block, preferred_element_type=jnp.float32).astype(jnp.bfloat16)
    cot_sum = jnp.dot(picked, cot_block, preferred_element_type=jnp.float32)
    return (token_sum, (slot_gate[:, None] * cot_sum).astype(jnp.bfloat16))


def expert_group(expert_rows, expert_cots, gate_weight, up_weight, down_weight):
    pre_gate = jnp.dot(expert_rows, gate_weight, preferred_element_type=jnp.float32)
    pre_up = jnp.dot(expert_rows, up_weight, preferred_element_type=jnp.float32)
    logistic = jax.nn.sigmoid(pre_gate)
    active = pre_gate * logistic
    hidden = (active * pre_up).astype(jnp.bfloat16)
    part_out = jnp.dot(hidden, down_weight, preferred_element_type=jnp.float32)
    grad_hidden = jnp.dot(expert_cots, down_weight.T, preferred_element_type=jnp.float32)
    grad_pre_gate = (grad_hidden * pre_up * logistic * (1.0 + pre_gate * (1.0 - logistic))).astype(
        jnp.bfloat16
    )
    grad_pre_up = (grad_hidden * active).astype(jnp.bfloat16)
    part_back = jnp.dot(grad_pre_gate, gate_weight.T, preferred_element_type=jnp.float32) + jnp.dot(
        grad_pre_up, up_weight.T, preferred_element_type=jnp.float32
    )
    grad_gate_w = jnp.dot(expert_rows.T, grad_pre_gate, preferred_element_type=jnp.float32).astype(
        jnp.bfloat16
    )
    grad_up_w = jnp.dot(expert_rows.T, grad_pre_up, preferred_element_type=jnp.float32).astype(
        jnp.bfloat16
    )
    grad_down_w = jnp.dot(hidden.T, expert_cots, preferred_element_type=jnp.float32).astype(
        jnp.bfloat16
    )
    return (part_out, part_back, (grad_gate_w, grad_up_w, grad_down_w))


def expert_group_t(expert_rows, expert_cots, gate_weight, up_weight, down_weight):
    pre_gate = jnp.dot(expert_rows, gate_weight, preferred_element_type=jnp.float32)
    pre_up = jnp.dot(expert_rows, up_weight, preferred_element_type=jnp.float32)
    logistic = jax.nn.sigmoid(pre_gate)
    active = pre_gate * logistic
    hidden = (active * pre_up).astype(jnp.bfloat16)
    pre_gate, pre_up, logistic, active, hidden = lax.optimization_barrier(
        (pre_gate, pre_up, logistic, active, hidden)
    )
    contract_h = (((1,), (1,)), ((), ()))
    out_t = lax.dot_general(
        down_weight.T, hidden, contract_h, preferred_element_type=jnp.float32
    ).astype(jnp.bfloat16)
    grad_hidden = jnp.dot(expert_cots, down_weight.T, preferred_element_type=jnp.float32)
    grad_pre_gate = (grad_hidden * pre_up * logistic * (1.0 + pre_gate * (1.0 - logistic))).astype(
        jnp.bfloat16
    )
    grad_pre_up = (grad_hidden * active).astype(jnp.bfloat16)
    back_t = (
        lax.dot_general(gate_weight, grad_pre_gate, contract_h, preferred_element_type=jnp.float32)
        + lax.dot_general(up_weight, grad_pre_up, contract_h, preferred_element_type=jnp.float32)
    ).astype(jnp.bfloat16)
    grad_gate_w = jnp.dot(expert_rows.T, grad_pre_gate, preferred_element_type=jnp.float32).astype(
        jnp.bfloat16
    )
    grad_up_w = jnp.dot(expert_rows.T, grad_pre_up, preferred_element_type=jnp.float32).astype(
        jnp.bfloat16
    )
    grad_down_w = jnp.dot(hidden.T, expert_cots, preferred_element_type=jnp.float32).astype(
        jnp.bfloat16
    )
    return (out_t, back_t, (grad_gate_w, grad_up_w, grad_down_w))


def local(
    tokens,
    cotangent,
    chosen_experts,
    chosen_slots,
    routing_gate_weight,
    padded_slot_count,
    w_gate,
    w_up,
    w_down,
):
    tok_rows, feature_width = tokens.shape
    per_token = chosen_experts.shape[1]
    expert_number = padded_slot_count.shape[1]
    expert_capacity = 2 * tok_rows * per_token // (OWNED * lax.axis_size("expert"))
    send_rows = expert_number * expert_capacity
    feature_share = feature_width // lax.axis_size("tensor")
    first_col = lax.axis_index("tensor") * feature_share
    slot_alive_mask, destination_slot = routing_layout(
        chosen_experts, chosen_slots, padded_slot_count[0], expert_capacity
    )
    local_tokens = lax.dynamic_slice_in_dim(tokens, first_col, feature_share, 1)
    local_cotangent_bf = lax.dynamic_slice_in_dim(cotangent, first_col, feature_share, 1)
    token_sum, cot_rows = pack_slots(
        local_tokens, local_cotangent_bf, routing_gate_weight, destination_slot, send_rows
    )
    rows_q = lax.all_to_all(
        token_sum.reshape(expert_number, expert_capacity, feature_share),
        "expert", split_axis=0, concat_axis=0, tiled=True,
    ).reshape(send_rows, feature_share)
    rows_q, cot_rows = lax.optimization_barrier((rows_q, cot_rows))
    rows_all = lax.all_gather(rows_q, "tensor", axis=1, tiled=True)
    cots_q = lax.all_to_all(
        cot_rows.reshape(expert_number, expert_capacity, feature_share),
        "expert", split_axis=0, concat_axis=0, tiled=True,
    ).reshape(send_rows, feature_share)
    cots_all = lax.all_gather(cots_q, "tensor", axis=1, tiled=True)
    out_t, back_t, grads = expert_group_t(
        rows_all, cots_all, w_gate[0], w_up[0], w_down[0]
    )
    total_out = lax.psum_scatter(out_t, "tensor", scatter_dimension=0, tiled=True)
    sources = total_out.shape[1] // expert_capacity
    came_out = lax.all_to_all(
        total_out.T.reshape(sources, expert_capacity, feature_share),
        "expert", split_axis=0, concat_axis=0, tiled=True,
    ).reshape(send_rows, feature_share)
    total_back = lax.psum_scatter(back_t, "tensor", scatter_dimension=0, tiled=True)
    came_back = lax.all_to_all(
        total_back.T.reshape(sources, expert_capacity, feature_share),
        "expert", split_axis=0, concat_axis=0, tiled=True,
    ).reshape(send_rows, feature_share)
    positions = jnp.maximum(destination_slot, 0).reshape(-1)
    out_rows = (
        jnp.take(came_out, positions, axis=0)
        .reshape(tok_rows, per_token, feature_share)
        .astype(jnp.float32)
    )
    returned_rows = (
        jnp.take(came_back, positions, axis=0)
        .reshape(tok_rows, per_token, feature_share)
        .astype(jnp.float32)
    )
    gate_scaling = jnp.where(slot_alive_mask, routing_gate_weight, 0.0)
    mixed = jnp.sum(gate_scaling[:, :, None] * out_rows, axis=1).astype(jnp.bfloat16)
    token_gradient = jnp.sum(
        jnp.where(slot_alive_mask[:, :, None], returned_rows, 0.0), axis=1
    ).astype(jnp.bfloat16)
    local_cotangent = local_cotangent_bf.astype(jnp.float32)
    hidden_totals = jnp.sum(local_cotangent[:, None, :] * out_rows, axis=2)
    gate_gradient = lax.psum(jnp.where(slot_alive_mask, hidden_totals, 0.0), "tensor")
    grad_gate_w, grad_up_w, grad_down_w = grads
    return (
        mixed,
        token_gradient,
        gate_gradient,
        grad_gate_w[None],
        grad_up_w[None],
        grad_down_w[None],
    )


def solution(mesh):
    in_specs = (
        P("expert", None),
        P("expert", None),
        P("expert", None),
        P("expert", None),
        P("expert", None),
        P("expert", None),
        P("expert", None, "tensor"),
        P("expert", None, "tensor"),
        P("expert", "tensor", None),
    )
    out_specs = (
        P("expert", "tensor"),
        P("expert", "tensor"),
        P("expert", None),
        P("expert", None, "tensor"),
        P("expert", None, "tensor"),
        P("expert", "tensor", None),
    )
    return jax.shard_map(local, mesh=mesh, in_specs=in_specs, out_specs=out_specs, check_vma=False)
```

```python
import jax
import jax.numpy as jnp
from jax import lax
from jax.sharding import PartitionSpec as P

OWNED = 4


def routing_layout(chosen_expert, chosen_slot, slot_count_row, expert_capacity):
    expert_number = slot_count_row.shape[0]
    one_hot = (
        chosen_expert[:, :, None] == jnp.arange(expert_number, dtype=jnp.int32)[None, None, :]
    ).astype(jnp.int32)
    slot_ceiling = jnp.sum(one_hot * slot_count_row[None, None, :], axis=2)
    slot_alive_mask = (chosen_expert < expert_number) & (chosen_slot < slot_ceiling)
    destination_slot = jnp.where(slot_alive_mask, chosen_expert * expert_capacity + chosen_slot, -1)
    return (slot_alive_mask, destination_slot)


def pack_slots(tok_block, cot_block, block_gates, destination_slot, send_rows):
    select = destination_slot[None, :, :] == jnp.arange(send_rows, dtype=jnp.int32)[:, None, None]
    picked = jnp.sum(select.astype(jnp.int32), axis=2).astype(jnp.bfloat16)
    slot_gate = jnp.sum(jnp.where(select, block_gates[None, :, :], 0.0), axis=(1, 2))
    token_sum = jnp.dot(picked, tok_block, preferred_element_type=jnp.float32).astype(jnp.bfloat16)
    cot_sum = jnp.dot(picked, cot_block, preferred_element_type=jnp.float32)
    return (token_sum, (slot_gate[:, None] * cot_sum).astype(jnp.bfloat16))


def expert_group(expert_rows, expert_cots, gate_weight, up_weight, down_weight):
    pre_gate = jnp.dot(expert_rows, gate_weight, preferred_element_type=jnp.float32)
    pre_up = jnp.dot(expert_rows, up_weight, preferred_element_type=jnp.float32)
    logistic = jax.nn.sigmoid(pre_gate)
    active = pre_gate * logistic
    hidden = (active * pre_up).astype(jnp.bfloat16)
    part_out = jnp.dot(hidden, down_weight, preferred_element_type=jnp.float32)
    grad_hidden = jnp.dot(expert_cots, down_weight.T, preferred_element_type=jnp.float32)
    grad_pre_gate = (grad_hidden * pre_up * logistic * (1.0 + pre_gate * (1.0 - logistic))).astype(
        jnp.bfloat16
    )
    grad_pre_up = (grad_hidden * active).astype(jnp.bfloat16)
    part_back = jnp.dot(grad_pre_gate, gate_weight.T, preferred_element_type=jnp.float32) + jnp.dot(
        grad_pre_up, up_weight.T, preferred_element_type=jnp.float32
    )
    grad_gate_w = jnp.dot(expert_rows.T, grad_pre_gate, preferred_element_type=jnp.float32).astype(
        jnp.bfloat16
    )
    grad_up_w = jnp.dot(expert_rows.T, grad_pre_up, preferred_element_type=jnp.float32).astype(
        jnp.bfloat16
    )
    grad_down_w = jnp.dot(hidden.T, expert_cots, preferred_element_type=jnp.float32).astype(
        jnp.bfloat16
    )
    return (part_out, part_back, (grad_gate_w, grad_up_w, grad_down_w))


def expert_group_t(expert_rows, expert_cots, gate_weight, up_weight, down_weight):
    pre_gate = jnp.dot(expert_rows, gate_weight, preferred_element_type=jnp.float32)
    pre_up = jnp.dot(expert_rows, up_weight, preferred_element_type=jnp.float32)
    logistic = jax.nn.sigmoid(pre_gate)
    active = pre_gate * logistic
    hidden = (active * pre_up).astype(jnp.bfloat16)
    pre_gate, pre_up, logistic, active, hidden = lax.optimization_barrier(
        (pre_gate, pre_up, logistic, active, hidden)
    )
    contract_h = (((1,), (1,)), ((), ()))
    out_t = lax.dot_general(
        down_weight.T, hidden, contract_h, preferred_element_type=jnp.float32
    ).astype(jnp.bfloat16)
    grad_hidden = jnp.dot(expert_cots, down_weight.T, preferred_element_type=jnp.float32)
    grad_pre_gate = (grad_hidden * pre_up * logistic * (1.0 + pre_gate * (1.0 - logistic))).astype(
        jnp.bfloat16
    )
    grad_pre_up = (grad_hidden * active).astype(jnp.bfloat16)
    back_t = (
        lax.dot_general(gate_weight, grad_pre_gate, contract_h, preferred_element_type=jnp.float32)
        + lax.dot_general(up_weight, grad_pre_up, contract_h, preferred_element_type=jnp.float32)
    ).astype(jnp.bfloat16)
    grad_gate_w = jnp.dot(expert_rows.T, grad_pre_gate, preferred_element_type=jnp.float32).astype(
        jnp.bfloat16
    )
    grad_up_w = jnp.dot(expert_rows.T, grad_pre_up, preferred_element_type=jnp.float32).astype(
        jnp.bfloat16
    )
    grad_down_w = jnp.dot(hidden.T, expert_cots, preferred_element_type=jnp.float32).astype(
        jnp.bfloat16
    )
    return (out_t, back_t, (grad_gate_w, grad_up_w, grad_down_w))


def local(
    tokens,
    cotangent,
    chosen_experts,
    chosen_slots,
    routing_gate_weight,
    padded_slot_count,
    w_gate,
    w_up,
    w_down,
):
    tok_rows, feature_width = tokens.shape
    per_token = chosen_experts.shape[1]
    expert_number = padded_slot_count.shape[1]
    expert_capacity = 2 * tok_rows * per_token // (OWNED * lax.axis_size("expert"))
    send_rows = expert_number * expert_capacity
    feature_share = feature_width // lax.axis_size("tensor")
    first_col = lax.axis_index("tensor") * feature_share
    slot_alive_mask, destination_slot = routing_layout(
        chosen_experts, chosen_slots, padded_slot_count[0], expert_capacity
    )
    local_tokens = lax.dynamic_slice_in_dim(tokens, first_col, feature_share, 1)
    local_cotangent_bf = lax.dynamic_slice_in_dim(cotangent, first_col, feature_share, 1)
    token_sum, _ = pack_slots(
        local_tokens, local_cotangent_bf[:, :0], routing_gate_weight, destination_slot, send_rows
    )
    _, cot_rows = pack_slots(
        tokens[:, :0], cotangent, routing_gate_weight, destination_slot, send_rows
    )
    rows_q = lax.all_to_all(
        token_sum.reshape(expert_number, expert_capacity, feature_share),
        "expert", split_axis=0, concat_axis=0, tiled=True,
    ).reshape(send_rows, feature_share)
    rows_q, cot_rows = lax.optimization_barrier((rows_q, cot_rows))
    rows_all = lax.all_gather(rows_q, "tensor", axis=1, tiled=True)
    cots_all = lax.all_to_all(
        cot_rows.reshape(expert_number, expert_capacity, feature_width),
        "expert", split_axis=0, concat_axis=0, tiled=True,
    ).reshape(send_rows, feature_width)
    out_t, back_t, grads = expert_group_t(
        rows_all, cots_all, w_gate[0], w_up[0], w_down[0]
    )
    total_out = lax.psum_scatter(out_t, "tensor", scatter_dimension=0, tiled=True)
    sources = total_out.shape[1] // expert_capacity
    came_out = lax.all_to_all(
        total_out.T.reshape(sources, expert_capacity, feature_share),
        "expert", split_axis=0, concat_axis=0, tiled=True,
    ).reshape(send_rows, feature_share)
    total_back = lax.psum_scatter(back_t, "tensor", scatter_dimension=0, tiled=True)
    came_back = lax.all_to_all(
        total_back.T.reshape(sources, expert_capacity, feature_share),
        "expert", split_axis=0, concat_axis=0, tiled=True,
    ).reshape(send_rows, feature_share)
    positions = jnp.maximum(destination_slot, 0).reshape(-1)
    out_rows = (
        jnp.take(came_out, positions, axis=0)
        .reshape(tok_rows, per_token, feature_share)
        .astype(jnp.float32)
    )
    returned_rows = (
        jnp.take(came_back, positions, axis=0)
        .reshape(tok_rows, per_token, feature_share)
        .astype(jnp.float32)
    )
    gate_scaling = jnp.where(slot_alive_mask, routing_gate_weight, 0.0)
    mixed = jnp.sum(gate_scaling[:, :, None] * out_rows, axis=1).astype(jnp.bfloat16)
    token_gradient = jnp.sum(
        jnp.where(slot_alive_mask[:, :, None], returned_rows, 0.0), axis=1
    ).astype(jnp.bfloat16)
    local_cotangent = local_cotangent_bf.astype(jnp.float32)
    hidden_totals = jnp.sum(local_cotangent[:, None, :] * out_rows, axis=2)
    gate_gradient = lax.psum(jnp.where(slot_alive_mask, hidden_totals, 0.0), "tensor")
    grad_gate_w, grad_up_w, grad_down_w = grads
    return (
        mixed,
        token_gradient,
        gate_gradient,
        grad_gate_w[None],
        grad_up_w[None],
        grad_down_w[None],
    )


def solution(mesh):
    in_specs = (
        P("expert", None),
        P("expert", None),
        P("expert", None),
        P("expert", None),
        P("expert", None),
        P("expert", None),
        P("expert", None, "tensor"),
        P("expert", None, "tensor"),
        P("expert", "tensor", None),
    )
    out_specs = (
        P("expert", "tensor"),
        P("expert", "tensor"),
        P("expert", None),
        P("expert", None, "tensor"),
        P("expert", None, "tensor"),
        P("expert", "tensor", None),
    )
    return jax.shard_map(local, mesh=mesh, in_specs=in_specs, out_specs=out_specs, check_vma=False)
```

```python
import jax
import jax.numpy as jnp
from jax import lax
from jax.sharding import PartitionSpec as P

OWNED = 4


def routing_layout(chosen_expert, chosen_slot, slot_count_row, expert_capacity):
    expert_number = slot_count_row.shape[0]
    one_hot = (
        chosen_expert[:, :, None] == jnp.arange(expert_number, dtype=jnp.int32)[None, None, :]
    ).astype(jnp.int32)
    slot_ceiling = jnp.sum(one_hot * slot_count_row[None, None, :], axis=2)
    slot_alive_mask = (chosen_expert < expert_number) & (chosen_slot < slot_ceiling)
    destination_slot = jnp.where(slot_alive_mask, chosen_expert * expert_capacity + chosen_slot, -1)
    return (slot_alive_mask, destination_slot)


def pack_slots(tok_block, cot_block, block_gates, destination_slot, send_rows):
    select = destination_slot[None, :, :] == jnp.arange(send_rows, dtype=jnp.int32)[:, None, None]
    picked = jnp.sum(select.astype(jnp.int32), axis=2).astype(jnp.bfloat16)
    slot_gate = jnp.sum(jnp.where(select, block_gates[None, :, :], 0.0), axis=(1, 2))
    token_sum = jnp.dot(picked, tok_block, preferred_element_type=jnp.float32).astype(jnp.bfloat16)
    cot_sum = jnp.dot(picked, cot_block, preferred_element_type=jnp.float32)
    return (token_sum, (slot_gate[:, None] * cot_sum).astype(jnp.bfloat16))


def expert_group(expert_rows, expert_cots, gate_weight, up_weight, down_weight):
    pre_gate = jnp.dot(expert_rows, gate_weight, preferred_element_type=jnp.float32)
    pre_up = jnp.dot(expert_rows, up_weight, preferred_element_type=jnp.float32)
    logistic = jax.nn.sigmoid(pre_gate)
    active = pre_gate * logistic
    hidden = (active * pre_up).astype(jnp.bfloat16)
    part_out = jnp.dot(hidden, down_weight, preferred_element_type=jnp.float32)
    grad_hidden = jnp.dot(expert_cots, down_weight.T, preferred_element_type=jnp.float32)
    grad_pre_gate = (grad_hidden * pre_up * logistic * (1.0 + pre_gate * (1.0 - logistic))).astype(
        jnp.bfloat16
    )
    grad_pre_up = (grad_hidden * active).astype(jnp.bfloat16)
    part_back = jnp.dot(grad_pre_gate, gate_weight.T, preferred_element_type=jnp.float32) + jnp.dot(
        grad_pre_up, up_weight.T, preferred_element_type=jnp.float32
    )
    grad_gate_w = jnp.dot(expert_rows.T, grad_pre_gate, preferred_element_type=jnp.float32).astype(
        jnp.bfloat16
    )
    grad_up_w = jnp.dot(expert_rows.T, grad_pre_up, preferred_element_type=jnp.float32).astype(
        jnp.bfloat16
    )
    grad_down_w = jnp.dot(hidden.T, expert_cots, preferred_element_type=jnp.float32).astype(
        jnp.bfloat16
    )
    return (part_out, part_back, (grad_gate_w, grad_up_w, grad_down_w))


def expert_group_t(expert_rows, expert_cots, gate_weight, up_weight, down_weight):
    pre_gate = jnp.dot(expert_rows, gate_weight, preferred_element_type=jnp.float32)
    pre_up = jnp.dot(expert_rows, up_weight, preferred_element_type=jnp.float32)
    logistic = jax.nn.sigmoid(pre_gate)
    active = pre_gate * logistic
    hidden = (active * pre_up).astype(jnp.bfloat16)
    pre_gate, pre_up, logistic, active, hidden = lax.optimization_barrier(
        (pre_gate, pre_up, logistic, active, hidden)
    )
    contract_h = (((1,), (1,)), ((), ()))
    out_t = lax.dot_general(
        down_weight.T, hidden, contract_h, preferred_element_type=jnp.float32
    ).astype(jnp.bfloat16)
    grad_hidden = jnp.dot(expert_cots, down_weight.T, preferred_element_type=jnp.float32)
    grad_pre_gate = (grad_hidden * pre_up * logistic * (1.0 + pre_gate * (1.0 - logistic))).astype(
        jnp.bfloat16
    )
    grad_pre_up = (grad_hidden * active).astype(jnp.bfloat16)
    back_t = (
        lax.dot_general(gate_weight, grad_pre_gate, contract_h, preferred_element_type=jnp.float32)
        + lax.dot_general(up_weight, grad_pre_up, contract_h, preferred_element_type=jnp.float32)
    ).astype(jnp.bfloat16)
    grad_gate_w = jnp.dot(expert_rows.T, grad_pre_gate, preferred_element_type=jnp.float32).astype(
        jnp.bfloat16
    )
    grad_up_w = jnp.dot(expert_rows.T, grad_pre_up, preferred_element_type=jnp.float32).astype(
        jnp.bfloat16
    )
    grad_down_w = jnp.dot(hidden.T, expert_cots, preferred_element_type=jnp.float32).astype(
        jnp.bfloat16
    )
    return (out_t, back_t, (grad_gate_w, grad_up_w, grad_down_w))


def local(
    tokens,
    cotangent,
    chosen_experts,
    chosen_slots,
    routing_gate_weight,
    padded_slot_count,
    w_gate,
    w_up,
    w_down,
):
    tok_rows, feature_width = tokens.shape
    per_token = chosen_experts.shape[1]
    expert_number = padded_slot_count.shape[1]
    expert_capacity = 2 * tok_rows * per_token // (OWNED * lax.axis_size("expert"))
    send_rows = expert_number * expert_capacity
    feature_share = feature_width // lax.axis_size("tensor")
    first_col = lax.axis_index("tensor") * feature_share
    slot_alive_mask, destination_slot = routing_layout(
        chosen_experts, chosen_slots, padded_slot_count[0], expert_capacity
    )
    local_tokens = lax.dynamic_slice_in_dim(tokens, first_col, feature_share, 1)
    local_cotangent_bf = lax.dynamic_slice_in_dim(cotangent, first_col, feature_share, 1)
    token_sum, _ = pack_slots(
        local_tokens, local_cotangent_bf[:, :0], routing_gate_weight, destination_slot, send_rows
    )
    _, cot_rows = pack_slots(
        tokens[:, :0], cotangent, routing_gate_weight, destination_slot, send_rows
    )
    rows_q = lax.all_to_all(
        token_sum.reshape(expert_number, expert_capacity, feature_share),
        "expert", split_axis=0, concat_axis=0, tiled=True,
    ).reshape(send_rows, feature_share)
    rows_q, cot_rows = lax.optimization_barrier((rows_q, cot_rows))
    rows_all = lax.all_gather(rows_q, "tensor", axis=1, tiled=True)
    cots_all = lax.all_to_all(
        cot_rows.reshape(expert_number, expert_capacity, feature_width),
        "expert", split_axis=0, concat_axis=0, tiled=True,
    ).reshape(send_rows, feature_width)
    out_t, back_t, grads = expert_group_t(
        rows_all, cots_all, w_gate[0], w_up[0], w_down[0]
    )
    total_out = lax.psum_scatter(out_t, "tensor", scatter_dimension=0, tiled=True)
    sources = total_out.shape[1] // expert_capacity
    came_out = lax.all_to_all(
        total_out.T.reshape(sources, expert_capacity, feature_share),
        "expert", split_axis=0, concat_axis=0, tiled=True,
    ).reshape(send_rows, feature_share)
    total_back = lax.psum_scatter(back_t, "tensor", scatter_dimension=0, tiled=True)
    came_back = lax.all_to_all(
        total_back.T.reshape(sources, expert_capacity, feature_share),
        "expert", split_axis=0, concat_axis=0, tiled=True,
    ).reshape(send_rows, feature_share)
    positions = jnp.maximum(destination_slot, 0).reshape(-1)
    out_rows = (
        jnp.take(came_out, positions, axis=0)
        .reshape(tok_rows, per_token, feature_share)
        .astype(jnp.float32)
    )
    gate_scaling = jnp.where(slot_alive_mask, routing_gate_weight, 0.0)
    mixed = jnp.sum(gate_scaling[:, :, None] * out_rows, axis=1).astype(jnp.bfloat16)
    route_hits = destination_slot[None, :, :] == jnp.arange(send_rows, dtype=jnp.int32)[:, None, None]
    slot_of_token = jnp.sum(route_hits.astype(jnp.int32), axis=2).astype(jnp.bfloat16)
    token_gradient = lax.dot_general(
        slot_of_token, came_back, (((0,), (0,)), ((), ())), preferred_element_type=jnp.float32
    ).astype(jnp.bfloat16)
    local_cotangent = local_cotangent_bf.astype(jnp.float32)
    hidden_totals = jnp.sum(local_cotangent[:, None, :] * out_rows, axis=2)
    gate_gradient = lax.psum(jnp.where(slot_alive_mask, hidden_totals, 0.0), "tensor")
    grad_gate_w, grad_up_w, grad_down_w = grads
    return (
        mixed,
        token_gradient,
        gate_gradient,
        grad_gate_w[None],
        grad_up_w[None],
        grad_down_w[None],
    )


def solution(mesh):
    in_specs = (
        P("expert", None),
        P("expert", None),
        P("expert", None),
        P("expert", None),
        P("expert", None),
        P("expert", None),
        P("expert", None, "tensor"),
        P("expert", None, "tensor"),
        P("expert", "tensor", None),
    )
    out_specs = (
        P("expert", "tensor"),
        P("expert", "tensor"),
        P("expert", None),
        P("expert", None, "tensor"),
        P("expert", None, "tensor"),
        P("expert", "tensor", None),
    )
    return jax.shard_map(local, mesh=mesh, in_specs=in_specs, out_specs=out_specs, check_vma=False)
```

```python
import jax
import jax.numpy as jnp
from jax import lax
from jax.sharding import PartitionSpec as P

OWNED = 4


def routing_layout(chosen_expert, chosen_slot, slot_count_row, expert_capacity):
    expert_number = slot_count_row.shape[0]
    one_hot = (
        chosen_expert[:, :, None] == jnp.arange(expert_number, dtype=jnp.int32)[None, None, :]
    ).astype(jnp.int32)
    slot_ceiling = jnp.sum(one_hot * slot_count_row[None, None, :], axis=2)
    slot_alive_mask = (chosen_expert < expert_number) & (chosen_slot < slot_ceiling)
    destination_slot = jnp.where(slot_alive_mask, chosen_expert * expert_capacity + chosen_slot, -1)
    return (slot_alive_mask, destination_slot)


def pack_slots(tok_block, cot_block, block_gates, destination_slot, send_rows):
    select = destination_slot[None, :, :] == jnp.arange(send_rows, dtype=jnp.int32)[:, None, None]
    picked = jnp.sum(select.astype(jnp.int32), axis=2).astype(jnp.bfloat16)
    slot_gate = jnp.sum(jnp.where(select, block_gates[None, :, :], 0.0), axis=(1, 2))
    token_sum = jnp.dot(picked, tok_block, preferred_element_type=jnp.float32).astype(jnp.bfloat16)
    cot_sum = jnp.dot(picked, cot_block, preferred_element_type=jnp.float32)
    return (token_sum, (slot_gate[:, None] * cot_sum).astype(jnp.bfloat16))


def expert_group(expert_rows, expert_cots, gate_weight, up_weight, down_weight):
    pre_gate = jnp.dot(expert_rows, gate_weight, preferred_element_type=jnp.float32)
    pre_up = jnp.dot(expert_rows, up_weight, preferred_element_type=jnp.float32)
    logistic = jax.nn.sigmoid(pre_gate)
    active = pre_gate * logistic
    hidden = (active * pre_up).astype(jnp.bfloat16)
    part_out = jnp.dot(hidden, down_weight, preferred_element_type=jnp.float32)
    grad_hidden = jnp.dot(expert_cots, down_weight.T, preferred_element_type=jnp.float32)
    grad_pre_gate = (grad_hidden * pre_up * logistic * (1.0 + pre_gate * (1.0 - logistic))).astype(
        jnp.bfloat16
    )
    grad_pre_up = (grad_hidden * active).astype(jnp.bfloat16)
    part_back = jnp.dot(grad_pre_gate, gate_weight.T, preferred_element_type=jnp.float32) + jnp.dot(
        grad_pre_up, up_weight.T, preferred_element_type=jnp.float32
    )
    grad_gate_w = jnp.dot(expert_rows.T, grad_pre_gate, preferred_element_type=jnp.float32).astype(
        jnp.bfloat16
    )
    grad_up_w = jnp.dot(expert_rows.T, grad_pre_up, preferred_element_type=jnp.float32).astype(
        jnp.bfloat16
    )
    grad_down_w = jnp.dot(hidden.T, expert_cots, preferred_element_type=jnp.float32).astype(
        jnp.bfloat16
    )
    return (part_out, part_back, (grad_gate_w, grad_up_w, grad_down_w))


def expert_group_t(expert_rows, expert_cots, gate_weight, up_weight, down_weight):
    pre_gate = jnp.dot(expert_rows, gate_weight, preferred_element_type=jnp.float32)
    pre_up = jnp.dot(expert_rows, up_weight, preferred_element_type=jnp.float32)
    logistic = jax.nn.sigmoid(pre_gate)
    active = pre_gate * logistic
    hidden = (active * pre_up).astype(jnp.bfloat16)
    pre_gate, pre_up, logistic, active, hidden = lax.optimization_barrier(
        (pre_gate, pre_up, logistic, active, hidden)
    )
    n_tensor = lax.axis_size("tensor")
    share = gate_weight.shape[0] // n_tensor
    down_parts = down_weight.reshape(down_weight.shape[0], n_tensor, share)
    out_t = jnp.einsum(
        "mh,hkd->kmd", hidden, down_parts, preferred_element_type=jnp.float32
    ).astype(jnp.bfloat16)
    grad_hidden = jnp.dot(expert_cots, down_weight.T, preferred_element_type=jnp.float32)
    grad_pre_gate = (grad_hidden * pre_up * logistic * (1.0 + pre_gate * (1.0 - logistic))).astype(
        jnp.bfloat16
    )
    grad_pre_up = (grad_hidden * active).astype(jnp.bfloat16)
    gate_parts = gate_weight.reshape(n_tensor, share, gate_weight.shape[1])
    up_parts = up_weight.reshape(n_tensor, share, up_weight.shape[1])
    back_t = (
        jnp.einsum("mh,kdh->kmd", grad_pre_gate, gate_parts, preferred_element_type=jnp.float32)
        + jnp.einsum("mh,kdh->kmd", grad_pre_up, up_parts, preferred_element_type=jnp.float32)
    ).astype(jnp.bfloat16)
    grad_gate_w = jnp.dot(expert_rows.T, grad_pre_gate, preferred_element_type=jnp.float32).astype(
        jnp.bfloat16
    )
    grad_up_w = jnp.dot(expert_rows.T, grad_pre_up, preferred_element_type=jnp.float32).astype(
        jnp.bfloat16
    )
    grad_down_w = jnp.dot(hidden.T, expert_cots, preferred_element_type=jnp.float32).astype(
        jnp.bfloat16
    )
    return (out_t, back_t, (grad_gate_w, grad_up_w, grad_down_w))


def local(
    tokens,
    cotangent,
    chosen_experts,
    chosen_slots,
    routing_gate_weight,
    padded_slot_count,
    w_gate,
    w_up,
    w_down,
):
    tok_rows, feature_width = tokens.shape
    per_token = chosen_experts.shape[1]
    expert_number = padded_slot_count.shape[1]
    expert_capacity = 2 * tok_rows * per_token // (OWNED * lax.axis_size("expert"))
    send_rows = expert_number * expert_capacity
    feature_share = feature_width // lax.axis_size("tensor")
    first_col = lax.axis_index("tensor") * feature_share
    slot_alive_mask, destination_slot = routing_layout(
        chosen_experts, chosen_slots, padded_slot_count[0], expert_capacity
    )
    local_tokens = lax.dynamic_slice_in_dim(tokens, first_col, feature_share, 1)
    local_cotangent_bf = lax.dynamic_slice_in_dim(cotangent, first_col, feature_share, 1)
    token_sum, _ = pack_slots(
        local_tokens, local_cotangent_bf[:, :0], routing_gate_weight, destination_slot, send_rows
    )
    _, cot_rows = pack_slots(
        tokens[:, :0], cotangent, routing_gate_weight, destination_slot, send_rows
    )
    rows_q = lax.all_to_all(
        token_sum.reshape(expert_number, expert_capacity, feature_share),
        "expert", split_axis=0, concat_axis=0, tiled=True,
    ).reshape(send_rows, feature_share)
    rows_q, cot_rows = lax.optimization_barrier((rows_q, cot_rows))
    rows_all = lax.all_gather(rows_q, "tensor", axis=1, tiled=True)
    cots_all = lax.all_to_all(
        cot_rows.reshape(expert_number, expert_capacity, feature_width),
        "expert", split_axis=0, concat_axis=0, tiled=True,
    ).reshape(send_rows, feature_width)
    out_t, back_t, grads = expert_group_t(
        rows_all, cots_all, w_gate[0], w_up[0], w_down[0]
    )
    total_out = lax.psum_scatter(out_t, "tensor", scatter_dimension=0, tiled=True)
    sources = total_out.shape[1] // expert_capacity
    came_out = lax.all_to_all(
        total_out.reshape(sources, expert_capacity, feature_share),
        "expert", split_axis=0, concat_axis=0, tiled=True,
    ).reshape(send_rows, feature_share)
    total_back = lax.psum_scatter(back_t, "tensor", scatter_dimension=0, tiled=True)
    came_back = lax.all_to_all(
        total_back.reshape(sources, expert_capacity, feature_share),
        "expert", split_axis=0, concat_axis=0, tiled=True,
    ).reshape(send_rows, feature_share)
    positions = jnp.maximum(destination_slot, 0).reshape(-1)
    out_rows = (
        jnp.take(came_out, positions, axis=0)
        .reshape(tok_rows, per_token, feature_share)
        .astype(jnp.float32)
    )
    gate_scaling = jnp.where(slot_alive_mask, routing_gate_weight, 0.0)
    mixed = jnp.sum(gate_scaling[:, :, None] * out_rows, axis=1).astype(jnp.bfloat16)
    route_hits = destination_slot[None, :, :] == jnp.arange(send_rows, dtype=jnp.int32)[:, None, None]
    slot_of_token = jnp.sum(route_hits.astype(jnp.int32), axis=2).astype(jnp.bfloat16)
    token_gradient = lax.dot_general(
        slot_of_token, came_back, (((0,), (0,)), ((), ())), preferred_element_type=jnp.float32
    ).astype(jnp.bfloat16)
    local_cotangent = local_cotangent_bf.astype(jnp.float32)
    hidden_totals = jnp.sum(local_cotangent[:, None, :] * out_rows, axis=2)
    gate_gradient = lax.psum(jnp.where(slot_alive_mask, hidden_totals, 0.0), "tensor")
    grad_gate_w, grad_up_w, grad_down_w = grads
    return (
        mixed,
        token_gradient,
        gate_gradient,
        grad_gate_w[None],
        grad_up_w[None],
        grad_down_w[None],
    )


def solution(mesh):
    in_specs = (
        P("expert", None),
        P("expert", None),
        P("expert", None),
        P("expert", None),
        P("expert", None),
        P("expert", None),
        P("expert", None, "tensor"),
        P("expert", None, "tensor"),
        P("expert", "tensor", None),
    )
    out_specs = (
        P("expert", "tensor"),
        P("expert", "tensor"),
        P("expert", None),
        P("expert", None, "tensor"),
        P("expert", None, "tensor"),
        P("expert", "tensor", None),
    )
    return jax.shard_map(local, mesh=mesh, in_specs=in_specs, out_specs=out_specs, check_vma=False)
```

```python
import jax
import jax.numpy as jnp
from jax import lax
from jax.sharding import PartitionSpec as P

OWNED = 4


def routing_layout(chosen_expert, chosen_slot, slot_count_row, expert_capacity):
    expert_number = slot_count_row.shape[0]
    one_hot = (
        chosen_expert[:, :, None] == jnp.arange(expert_number, dtype=jnp.int32)[None, None, :]
    ).astype(jnp.int32)
    slot_ceiling = jnp.sum(one_hot * slot_count_row[None, None, :], axis=2)
    slot_alive_mask = (chosen_expert < expert_number) & (chosen_slot < slot_ceiling)
    destination_slot = jnp.where(slot_alive_mask, chosen_expert * expert_capacity + chosen_slot, -1)
    return (slot_alive_mask, destination_slot)


def pack_slots(tok_block, cot_block, block_gates, destination_slot, send_rows):
    select = destination_slot[None, :, :] == jnp.arange(send_rows, dtype=jnp.int32)[:, None, None]
    picked = jnp.sum(select.astype(jnp.int32), axis=2).astype(jnp.bfloat16)
    slot_gate = jnp.sum(jnp.where(select, block_gates[None, :, :], 0.0), axis=(1, 2))
    token_sum = jnp.dot(picked, tok_block, preferred_element_type=jnp.float32).astype(jnp.bfloat16)
    cot_sum = jnp.dot(picked, cot_block, preferred_element_type=jnp.float32)
    return (token_sum, (slot_gate[:, None] * cot_sum).astype(jnp.bfloat16))


def expert_group(expert_rows, expert_cots, gate_weight, up_weight, down_weight):
    pre_gate = jnp.dot(expert_rows, gate_weight, preferred_element_type=jnp.float32)
    pre_up = jnp.dot(expert_rows, up_weight, preferred_element_type=jnp.float32)
    logistic = jax.nn.sigmoid(pre_gate)
    active = pre_gate * logistic
    hidden = (active * pre_up).astype(jnp.bfloat16)
    part_out = jnp.dot(hidden, down_weight, preferred_element_type=jnp.float32)
    grad_hidden = jnp.dot(expert_cots, down_weight.T, preferred_element_type=jnp.float32)
    grad_pre_gate = (grad_hidden * pre_up * logistic * (1.0 + pre_gate * (1.0 - logistic))).astype(
        jnp.bfloat16
    )
    grad_pre_up = (grad_hidden * active).astype(jnp.bfloat16)
    part_back = jnp.dot(grad_pre_gate, gate_weight.T, preferred_element_type=jnp.float32) + jnp.dot(
        grad_pre_up, up_weight.T, preferred_element_type=jnp.float32
    )
    grad_gate_w = jnp.dot(expert_rows.T, grad_pre_gate, preferred_element_type=jnp.float32).astype(
        jnp.bfloat16
    )
    grad_up_w = jnp.dot(expert_rows.T, grad_pre_up, preferred_element_type=jnp.float32).astype(
        jnp.bfloat16
    )
    grad_down_w = jnp.dot(hidden.T, expert_cots, preferred_element_type=jnp.float32).astype(
        jnp.bfloat16
    )
    return (part_out, part_back, (grad_gate_w, grad_up_w, grad_down_w))


def expert_group_t(expert_rows, expert_cots, gate_weight, up_weight, down_weight):
    pre_gate = jnp.dot(expert_rows, gate_weight, preferred_element_type=jnp.float32)
    pre_up = jnp.dot(expert_rows, up_weight, preferred_element_type=jnp.float32)
    logistic = jax.nn.sigmoid(pre_gate)
    active = pre_gate * logistic
    hidden = (active * pre_up).astype(jnp.bfloat16)
    pre_gate, pre_up, logistic, active, hidden = lax.optimization_barrier(
        (pre_gate, pre_up, logistic, active, hidden)
    )
    n_tensor = lax.axis_size("tensor")
    share = gate_weight.shape[0] // n_tensor
    down_parts = down_weight.reshape(down_weight.shape[0], n_tensor, share)
    out_t = jnp.einsum(
        "mh,hkd->kmd", hidden, down_parts, preferred_element_type=jnp.float32
    ).astype(jnp.bfloat16)
    grad_hidden = jnp.dot(expert_cots, down_weight.T, preferred_element_type=jnp.float32)
    grad_pre_gate = (grad_hidden * pre_up * logistic * (1.0 + pre_gate * (1.0 - logistic))).astype(
        jnp.bfloat16
    )
    grad_pre_up = (grad_hidden * active).astype(jnp.bfloat16)
    grad_gate_w = jnp.dot(expert_rows.T, grad_pre_gate, preferred_element_type=jnp.float32).astype(
        jnp.bfloat16
    )
    grad_up_w = jnp.dot(expert_rows.T, grad_pre_up, preferred_element_type=jnp.float32).astype(
        jnp.bfloat16
    )
    grad_down_w = jnp.dot(hidden.T, expert_cots, preferred_element_type=jnp.float32).astype(
        jnp.bfloat16
    )
    return (out_t, (grad_pre_gate, grad_pre_up), (grad_gate_w, grad_up_w, grad_down_w))


def local(
    tokens,
    cotangent,
    chosen_experts,
    chosen_slots,
    routing_gate_weight,
    padded_slot_count,
    w_gate,
    w_up,
    w_down,
):
    tok_rows, feature_width = tokens.shape
    per_token = chosen_experts.shape[1]
    expert_number = padded_slot_count.shape[1]
    expert_capacity = 2 * tok_rows * per_token // (OWNED * lax.axis_size("expert"))
    send_rows = expert_number * expert_capacity
    feature_share = feature_width // lax.axis_size("tensor")
    first_col = lax.axis_index("tensor") * feature_share
    slot_alive_mask, destination_slot = routing_layout(
        chosen_experts, chosen_slots, padded_slot_count[0], expert_capacity
    )
    n_tensor = lax.axis_size("tensor")
    me = lax.axis_index("tensor")
    weight_parts = jnp.stack(
        [
            w_gate[0].reshape(n_tensor, feature_share, w_gate.shape[2]),
            w_up[0].reshape(n_tensor, feature_share, w_up.shape[2]),
        ],
        axis=1,
    )
    by_shift = [lax.dynamic_index_in_dim(weight_parts, me, 0, keepdims=False)]
    for shift in range(1, n_tensor):
        outgoing = lax.dynamic_index_in_dim(weight_parts, (me + shift) % n_tensor, 0, keepdims=False)
        by_shift.append(
            lax.ppermute(outgoing, "tensor", [(i, (i + shift) % n_tensor) for i in range(n_tensor)])
        )
    source_of_shift = (me - jnp.arange(n_tensor)) % n_tensor
    local_tokens = lax.dynamic_slice_in_dim(tokens, first_col, feature_share, 1)
    local_cotangent_bf = lax.dynamic_slice_in_dim(cotangent, first_col, feature_share, 1)
    token_sum, _ = pack_slots(
        local_tokens, local_cotangent_bf[:, :0], routing_gate_weight, destination_slot, send_rows
    )
    _, cot_rows = pack_slots(
        tokens[:, :0], cotangent, routing_gate_weight, destination_slot, send_rows
    )
    rows_q = lax.all_to_all(
        token_sum.reshape(expert_number, expert_capacity, feature_share),
        "expert", split_axis=0, concat_axis=0, tiled=True,
    ).reshape(send_rows, feature_share)
    rows_q, cot_rows, by_shift = lax.optimization_barrier((rows_q, cot_rows, by_shift))
    swapped = jnp.stack(by_shift)
    rows_all = lax.all_gather(rows_q, "tensor", axis=1, tiled=True)
    cots_all = lax.all_to_all(
        cot_rows.reshape(expert_number, expert_capacity, feature_width),
        "expert", split_axis=0, concat_axis=0, tiled=True,
    ).reshape(send_rows, feature_width)
    out_t, grads_pre, grads = expert_group_t(
        rows_all, cots_all, w_gate[0], w_up[0], w_down[0]
    )
    total_out = lax.psum_scatter(out_t, "tensor", scatter_dimension=0, tiled=True)
    total_out, grads_pre = lax.optimization_barrier((total_out, grads_pre))
    sources = total_out.shape[1] // expert_capacity
    came_out = lax.all_to_all(
        total_out.reshape(sources, expert_capacity, feature_share),
        "expert", split_axis=0, concat_axis=0, tiled=True,
    ).reshape(send_rows, feature_share)
    grad_all = jnp.take(
        lax.all_gather(jnp.stack(grads_pre), "tensor", axis=1, tiled=False),
        source_of_shift,
        axis=1,
    )
    total_back = (
        jnp.einsum("kmh,kdh->md", grad_all[0], swapped[:, 0], preferred_element_type=jnp.float32)
        + jnp.einsum("kmh,kdh->md", grad_all[1], swapped[:, 1], preferred_element_type=jnp.float32)
    ).astype(jnp.bfloat16)
    came_back = lax.all_to_all(
        total_back.reshape(sources, expert_capacity, feature_share),
        "expert", split_axis=0, concat_axis=0, tiled=True,
    ).reshape(send_rows, feature_share)
    positions = jnp.maximum(destination_slot, 0).reshape(-1)
    out_rows = (
        jnp.take(came_out, positions, axis=0)
        .reshape(tok_rows, per_token, feature_share)
        .astype(jnp.float32)
    )
    gate_scaling = jnp.where(slot_alive_mask, routing_gate_weight, 0.0)
    mixed = jnp.sum(gate_scaling[:, :, None] * out_rows, axis=1).astype(jnp.bfloat16)
    route_hits = destination_slot[None, :, :] == jnp.arange(send_rows, dtype=jnp.int32)[:, None, None]
    slot_of_token = jnp.sum(route_hits.astype(jnp.int32), axis=2).astype(jnp.bfloat16)
    token_gradient = lax.dot_general(
        slot_of_token, came_back, (((0,), (0,)), ((), ())), preferred_element_type=jnp.float32
    ).astype(jnp.bfloat16)
    local_cotangent = local_cotangent_bf.astype(jnp.float32)
    hidden_totals = jnp.sum(local_cotangent[:, None, :] * out_rows, axis=2)
    gate_gradient = lax.psum(jnp.where(slot_alive_mask, hidden_totals, 0.0), "tensor")
    grad_gate_w, grad_up_w, grad_down_w = grads
    return (
        mixed,
        token_gradient,
        gate_gradient,
        grad_gate_w[None],
        grad_up_w[None],
        grad_down_w[None],
    )


def solution(mesh):
    in_specs = (
        P("expert", None),
        P("expert", None),
        P("expert", None),
        P("expert", None),
        P("expert", None),
        P("expert", None),
        P("expert", None, "tensor"),
        P("expert", None, "tensor"),
        P("expert", "tensor", None),
    )
    out_specs = (
        P("expert", "tensor"),
        P("expert", "tensor"),
        P("expert", None),
        P("expert", None, "tensor"),
        P("expert", None, "tensor"),
        P("expert", "tensor", None),
    )
    return jax.shard_map(local, mesh=mesh, in_specs=in_specs, out_specs=out_specs, check_vma=False)
```

```python
import jax
import jax.numpy as jnp
from jax import lax
from jax.sharding import PartitionSpec as P

OWNED = 4


def routing_layout(chosen_expert, chosen_slot, slot_count_row, expert_capacity):
    expert_number = slot_count_row.shape[0]
    one_hot = (
        chosen_expert[:, :, None] == jnp.arange(expert_number, dtype=jnp.int32)[None, None, :]
    ).astype(jnp.int32)
    slot_ceiling = jnp.sum(one_hot * slot_count_row[None, None, :], axis=2)
    slot_alive_mask = (chosen_expert < expert_number) & (chosen_slot < slot_ceiling)
    destination_slot = jnp.where(slot_alive_mask, chosen_expert * expert_capacity + chosen_slot, -1)
    return (slot_alive_mask, destination_slot)


def pack_slots(tok_block, cot_block, block_gates, destination_slot, send_rows):
    select = destination_slot[None, :, :] == jnp.arange(send_rows, dtype=jnp.int32)[:, None, None]
    picked = jnp.sum(select.astype(jnp.int32), axis=2).astype(jnp.bfloat16)
    slot_gate = jnp.sum(jnp.where(select, block_gates[None, :, :], 0.0), axis=(1, 2))
    token_sum = jnp.dot(picked, tok_block, preferred_element_type=jnp.float32).astype(jnp.bfloat16)
    cot_sum = jnp.dot(picked, cot_block, preferred_element_type=jnp.float32)
    return (token_sum, (slot_gate[:, None] * cot_sum).astype(jnp.bfloat16))


def expert_group(expert_rows, expert_cots, gate_weight, up_weight, down_weight):
    pre_gate = jnp.dot(expert_rows, gate_weight, preferred_element_type=jnp.float32)
    pre_up = jnp.dot(expert_rows, up_weight, preferred_element_type=jnp.float32)
    logistic = jax.nn.sigmoid(pre_gate)
    active = pre_gate * logistic
    hidden = (active * pre_up).astype(jnp.bfloat16)
    part_out = jnp.dot(hidden, down_weight, preferred_element_type=jnp.float32)
    grad_hidden = jnp.dot(expert_cots, down_weight.T, preferred_element_type=jnp.float32)
    grad_pre_gate = (grad_hidden * pre_up * logistic * (1.0 + pre_gate * (1.0 - logistic))).astype(
        jnp.bfloat16
    )
    grad_pre_up = (grad_hidden * active).astype(jnp.bfloat16)
    part_back = jnp.dot(grad_pre_gate, gate_weight.T, preferred_element_type=jnp.float32) + jnp.dot(
        grad_pre_up, up_weight.T, preferred_element_type=jnp.float32
    )
    grad_gate_w = jnp.dot(expert_rows.T, grad_pre_gate, preferred_element_type=jnp.float32).astype(
        jnp.bfloat16
    )
    grad_up_w = jnp.dot(expert_rows.T, grad_pre_up, preferred_element_type=jnp.float32).astype(
        jnp.bfloat16
    )
    grad_down_w = jnp.dot(hidden.T, expert_cots, preferred_element_type=jnp.float32).astype(
        jnp.bfloat16
    )
    return (part_out, part_back, (grad_gate_w, grad_up_w, grad_down_w))


def expert_group_t(expert_rows, expert_cots, gate_weight, up_weight, down_weight):
    n_tensor = expert_rows.shape[0]
    share = expert_rows.shape[2]
    gate_parts = gate_weight.reshape(n_tensor, share, gate_weight.shape[1])
    up_parts = up_weight.reshape(n_tensor, share, up_weight.shape[1])
    pre_gate = jnp.einsum("kmd,kdh->mh", expert_rows, gate_parts, preferred_element_type=jnp.float32)
    pre_up = jnp.einsum("kmd,kdh->mh", expert_rows, up_parts, preferred_element_type=jnp.float32)
    logistic = jax.nn.sigmoid(pre_gate)
    active = pre_gate * logistic
    hidden = (active * pre_up).astype(jnp.bfloat16)
    pre_gate, pre_up, logistic, active, hidden = lax.optimization_barrier(
        (pre_gate, pre_up, logistic, active, hidden)
    )
    down_parts = down_weight.reshape(down_weight.shape[0], n_tensor, share)
    out_t = jnp.einsum(
        "mh,hkd->kmd", hidden, down_parts, preferred_element_type=jnp.float32
    ).astype(jnp.bfloat16)
    grad_hidden = jnp.dot(expert_cots, down_weight.T, preferred_element_type=jnp.float32)
    grad_pre_gate = (grad_hidden * pre_up * logistic * (1.0 + pre_gate * (1.0 - logistic))).astype(
        jnp.bfloat16
    )
    grad_pre_up = (grad_hidden * active).astype(jnp.bfloat16)
    back_t = (
        jnp.einsum("mh,kdh->kmd", grad_pre_gate, gate_parts, preferred_element_type=jnp.float32)
        + jnp.einsum("mh,kdh->kmd", grad_pre_up, up_parts, preferred_element_type=jnp.float32)
    ).astype(jnp.bfloat16)
    grad_gate_w = (
        jnp.einsum("kmd,mh->kdh", expert_rows, grad_pre_gate, preferred_element_type=jnp.float32)
        .astype(jnp.bfloat16)
        .reshape(gate_weight.shape)
    )
    grad_up_w = (
        jnp.einsum("kmd,mh->kdh", expert_rows, grad_pre_up, preferred_element_type=jnp.float32)
        .astype(jnp.bfloat16)
        .reshape(up_weight.shape)
    )
    grad_down_w = jnp.dot(hidden.T, expert_cots, preferred_element_type=jnp.float32).astype(
        jnp.bfloat16
    )
    return (out_t, back_t, (grad_gate_w, grad_up_w, grad_down_w))


def local(
    tokens,
    cotangent,
    chosen_experts,
    chosen_slots,
    routing_gate_weight,
    padded_slot_count,
    w_gate,
    w_up,
    w_down,
):
    tok_rows, feature_width = tokens.shape
    per_token = chosen_experts.shape[1]
    expert_number = padded_slot_count.shape[1]
    expert_capacity = 2 * tok_rows * per_token // (OWNED * lax.axis_size("expert"))
    send_rows = expert_number * expert_capacity
    feature_share = feature_width // lax.axis_size("tensor")
    first_col = lax.axis_index("tensor") * feature_share
    slot_alive_mask, destination_slot = routing_layout(
        chosen_experts, chosen_slots, padded_slot_count[0], expert_capacity
    )
    local_tokens = lax.dynamic_slice_in_dim(tokens, first_col, feature_share, 1)
    local_cotangent_bf = lax.dynamic_slice_in_dim(cotangent, first_col, feature_share, 1)
    token_sum, _ = pack_slots(
        local_tokens, local_cotangent_bf[:, :0], routing_gate_weight, destination_slot, send_rows
    )
    _, cot_rows = pack_slots(
        tokens[:, :0], cotangent, routing_gate_weight, destination_slot, send_rows
    )
    rows_q = lax.all_to_all(
        token_sum.reshape(expert_number, expert_capacity, feature_share),
        "expert", split_axis=0, concat_axis=0, tiled=True,
    ).reshape(send_rows, feature_share)
    rows_q, cot_rows = lax.optimization_barrier((rows_q, cot_rows))
    rows_all = lax.all_gather(rows_q, "tensor", axis=0, tiled=False)
    cots_all = lax.all_to_all(
        cot_rows.reshape(expert_number, expert_capacity, feature_width),
        "expert", split_axis=0, concat_axis=0, tiled=True,
    ).reshape(send_rows, feature_width)
    out_t, back_t, grads = expert_group_t(
        rows_all, cots_all, w_gate[0], w_up[0], w_down[0]
    )
    total_out = lax.psum_scatter(out_t, "tensor", scatter_dimension=0, tiled=True)
    sources = total_out.shape[1] // expert_capacity
    came_out = lax.all_to_all(
        total_out.reshape(sources, expert_capacity, feature_share),
        "expert", split_axis=0, concat_axis=0, tiled=True,
    ).reshape(send_rows, feature_share)
    total_back = lax.psum_scatter(back_t, "tensor", scatter_dimension=0, tiled=True)
    came_back = lax.all_to_all(
        total_back.reshape(sources, expert_capacity, feature_share),
        "expert", split_axis=0, concat_axis=0, tiled=True,
    ).reshape(send_rows, feature_share)
    positions = jnp.maximum(destination_slot, 0).reshape(-1)
    out_rows = (
        jnp.take(came_out, positions, axis=0)
        .reshape(tok_rows, per_token, feature_share)
        .astype(jnp.float32)
    )
    gate_scaling = jnp.where(slot_alive_mask, routing_gate_weight, 0.0)
    mixed = jnp.sum(gate_scaling[:, :, None] * out_rows, axis=1).astype(jnp.bfloat16)
    route_hits = destination_slot[None, :, :] == jnp.arange(send_rows, dtype=jnp.int32)[:, None, None]
    slot_of_token = jnp.sum(route_hits.astype(jnp.int32), axis=2).astype(jnp.bfloat16)
    token_gradient = lax.dot_general(
        slot_of_token, came_back, (((0,), (0,)), ((), ())), preferred_element_type=jnp.float32
    ).astype(jnp.bfloat16)
    local_cotangent = local_cotangent_bf.astype(jnp.float32)
    hidden_totals = jnp.sum(local_cotangent[:, None, :] * out_rows, axis=2)
    gate_gradient = lax.psum(jnp.where(slot_alive_mask, hidden_totals, 0.0), "tensor")
    grad_gate_w, grad_up_w, grad_down_w = grads
    return (
        mixed,
        token_gradient,
        gate_gradient,
        grad_gate_w[None],
        grad_up_w[None],
        grad_down_w[None],
    )


def solution(mesh):
    in_specs = (
        P("expert", None),
        P("expert", None),
        P("expert", None),
        P("expert", None),
        P("expert", None),
        P("expert", None),
        P("expert", None, "tensor"),
        P("expert", None, "tensor"),
        P("expert", "tensor", None),
    )
    out_specs = (
        P("expert", "tensor"),
        P("expert", "tensor"),
        P("expert", None),
        P("expert", None, "tensor"),
        P("expert", None, "tensor"),
        P("expert", "tensor", None),
    )
    return jax.shard_map(local, mesh=mesh, in_specs=in_specs, out_specs=out_specs, check_vma=False)
```

```python
import jax
import jax.numpy as jnp
from jax import lax
from jax.sharding import PartitionSpec as P

OWNED = 4


def routing_layout(chosen_expert, chosen_slot, slot_count_row, expert_capacity):
    expert_number = slot_count_row.shape[0]
    one_hot = (
        chosen_expert[:, :, None] == jnp.arange(expert_number, dtype=jnp.int32)[None, None, :]
    ).astype(jnp.int32)
    slot_ceiling = jnp.sum(one_hot * slot_count_row[None, None, :], axis=2)
    slot_alive_mask = (chosen_expert < expert_number) & (chosen_slot < slot_ceiling)
    destination_slot = jnp.where(slot_alive_mask, chosen_expert * expert_capacity + chosen_slot, -1)
    return (slot_alive_mask, destination_slot)


def pack_slots(tok_block, cot_block, block_gates, destination_slot, send_rows):
    select = destination_slot[None, :, :] == jnp.arange(send_rows, dtype=jnp.int32)[:, None, None]
    picked = jnp.sum(select.astype(jnp.int32), axis=2).astype(jnp.bfloat16)
    slot_gate = jnp.sum(jnp.where(select, block_gates[None, :, :], 0.0), axis=(1, 2))
    token_sum = jnp.dot(picked, tok_block, preferred_element_type=jnp.float32).astype(jnp.bfloat16)
    cot_sum = jnp.dot(picked, cot_block, preferred_element_type=jnp.float32)
    return (token_sum, (slot_gate[:, None] * cot_sum).astype(jnp.bfloat16))


def expert_group(expert_rows, expert_cots, gate_weight, up_weight, down_weight):
    pre_gate = jnp.dot(expert_rows, gate_weight, preferred_element_type=jnp.float32)
    pre_up = jnp.dot(expert_rows, up_weight, preferred_element_type=jnp.float32)
    logistic = jax.nn.sigmoid(pre_gate)
    active = pre_gate * logistic
    hidden = (active * pre_up).astype(jnp.bfloat16)
    part_out = jnp.dot(hidden, down_weight, preferred_element_type=jnp.float32)
    grad_hidden = jnp.dot(expert_cots, down_weight.T, preferred_element_type=jnp.float32)
    grad_pre_gate = (grad_hidden * pre_up * logistic * (1.0 + pre_gate * (1.0 - logistic))).astype(
        jnp.bfloat16
    )
    grad_pre_up = (grad_hidden * active).astype(jnp.bfloat16)
    part_back = jnp.dot(grad_pre_gate, gate_weight.T, preferred_element_type=jnp.float32) + jnp.dot(
        grad_pre_up, up_weight.T, preferred_element_type=jnp.float32
    )
    grad_gate_w = jnp.dot(expert_rows.T, grad_pre_gate, preferred_element_type=jnp.float32).astype(
        jnp.bfloat16
    )
    grad_up_w = jnp.dot(expert_rows.T, grad_pre_up, preferred_element_type=jnp.float32).astype(
        jnp.bfloat16
    )
    grad_down_w = jnp.dot(hidden.T, expert_cots, preferred_element_type=jnp.float32).astype(
        jnp.bfloat16
    )
    return (part_out, part_back, (grad_gate_w, grad_up_w, grad_down_w))


def expert_group_t(expert_rows, expert_cots, gate_weight, up_weight, down_weight):
    pre_gate = jnp.dot(expert_rows, gate_weight, preferred_element_type=jnp.float32)
    pre_up = jnp.dot(expert_rows, up_weight, preferred_element_type=jnp.float32)
    logistic = jax.nn.sigmoid(pre_gate)
    active = pre_gate * logistic
    hidden = (active * pre_up).astype(jnp.bfloat16)
    pre_gate, pre_up, logistic, active, hidden = lax.optimization_barrier(
        (pre_gate, pre_up, logistic, active, hidden)
    )
    n_tensor = lax.axis_size("tensor")
    share = gate_weight.shape[0] // n_tensor
    down_parts = down_weight.reshape(down_weight.shape[0], n_tensor, share)
    out_t = jnp.einsum(
        "mh,hkd->kmd", hidden, down_parts, preferred_element_type=jnp.float32
    ).astype(jnp.bfloat16)
    grad_hidden = jnp.dot(expert_cots, down_weight.T, preferred_element_type=jnp.float32)
    grad_pre_gate = (grad_hidden * pre_up * logistic * (1.0 + pre_gate * (1.0 - logistic))).astype(
        jnp.bfloat16
    )
    grad_pre_up = (grad_hidden * active).astype(jnp.bfloat16)
    gate_parts = gate_weight.reshape(n_tensor, share, gate_weight.shape[1])
    up_parts = up_weight.reshape(n_tensor, share, up_weight.shape[1])
    back_t = (
        jnp.einsum("mh,kdh->kmd", grad_pre_gate, gate_parts, preferred_element_type=jnp.float32)
        + jnp.einsum("mh,kdh->kmd", grad_pre_up, up_parts, preferred_element_type=jnp.float32)
    ).astype(jnp.bfloat16)
    grad_gate_w = jnp.dot(expert_rows.T, grad_pre_gate, preferred_element_type=jnp.float32).astype(
        jnp.bfloat16
    )
    grad_up_w = jnp.dot(expert_rows.T, grad_pre_up, preferred_element_type=jnp.float32).astype(
        jnp.bfloat16
    )
    grad_down_w = jnp.dot(hidden.T, expert_cots, preferred_element_type=jnp.float32).astype(
        jnp.bfloat16
    )
    return (out_t, back_t, (grad_gate_w, grad_up_w, grad_down_w))


def local(
    tokens,
    cotangent,
    chosen_experts,
    chosen_slots,
    routing_gate_weight,
    padded_slot_count,
    w_gate,
    w_up,
    w_down,
):
    tok_rows, feature_width = tokens.shape
    per_token = chosen_experts.shape[1]
    expert_number = padded_slot_count.shape[1]
    expert_capacity = 2 * tok_rows * per_token // (OWNED * lax.axis_size("expert"))
    send_rows = expert_number * expert_capacity
    feature_share = feature_width // lax.axis_size("tensor")
    first_col = lax.axis_index("tensor") * feature_share
    slot_alive_mask, destination_slot = routing_layout(
        chosen_experts, chosen_slots, padded_slot_count[0], expert_capacity
    )
    local_tokens = lax.dynamic_slice_in_dim(tokens, first_col, feature_share, 1)
    local_cotangent_bf = lax.dynamic_slice_in_dim(cotangent, first_col, feature_share, 1)
    token_sum, _ = pack_slots(
        local_tokens, local_cotangent_bf[:, :0], routing_gate_weight, destination_slot, send_rows
    )
    _, cot_rows = pack_slots(
        tokens[:, :0], cotangent, routing_gate_weight, destination_slot, send_rows
    )
    rows_q = lax.all_to_all(
        token_sum.reshape(expert_number, expert_capacity, feature_share),
        "expert", split_axis=0, concat_axis=0, tiled=True,
    ).reshape(send_rows, feature_share)
    rows_q, cot_rows = lax.optimization_barrier((rows_q, cot_rows))
    rows_all = lax.all_gather(rows_q, "tensor", axis=1, tiled=True)
    cots_all = lax.all_to_all(
        cot_rows.reshape(expert_number, expert_capacity, feature_width),
        "expert", split_axis=0, concat_axis=0, tiled=True,
    ).reshape(send_rows, feature_width)
    out_t, back_t, grads = expert_group_t(
        rows_all, cots_all, w_gate[0], w_up[0], w_down[0]
    )
    total_out = lax.psum_scatter(out_t, "tensor", scatter_dimension=0, tiled=True)
    total_out, back_t = lax.optimization_barrier((total_out, back_t))
    sources = total_out.shape[1] // expert_capacity
    came_out = lax.all_to_all(
        total_out.reshape(sources, expert_capacity, feature_share),
        "expert", split_axis=0, concat_axis=0, tiled=True,
    ).reshape(send_rows, feature_share)
    ring_cols = 4 * 128
    sc_part = lax.psum_scatter(back_t[:, :, ring_cols:], "tensor", scatter_dimension=0, tiled=True)
    ring_in = back_t[:, :, :ring_cols]
    n_tensor = ring_in.shape[0]
    me = lax.axis_index("tensor")
    reverse = [(i, (i - 1) % n_tensor) for i in range(n_tensor)]
    acc = lax.dynamic_index_in_dim(ring_in, (me + 1) % n_tensor, 0, keepdims=False)
    for step in range(1, n_tensor):
        moved = lax.ppermute(acc, "tensor", reverse)
        mine = lax.dynamic_index_in_dim(ring_in, (me + 1 + step) % n_tensor, 0, keepdims=False)
        acc = (moved.astype(jnp.float32) + mine.astype(jnp.float32)).astype(jnp.bfloat16)
    total_back = jnp.concatenate([acc, sc_part[0]], axis=1)
    came_back = lax.all_to_all(
        total_back.reshape(sources, expert_capacity, feature_share),
        "expert", split_axis=0, concat_axis=0, tiled=True,
    ).reshape(send_rows, feature_share)
    positions = jnp.maximum(destination_slot, 0).reshape(-1)
    out_rows = (
        jnp.take(came_out, positions, axis=0)
        .reshape(tok_rows, per_token, feature_share)
        .astype(jnp.float32)
    )
    gate_scaling = jnp.where(slot_alive_mask, routing_gate_weight, 0.0)
    mixed = jnp.sum(gate_scaling[:, :, None] * out_rows, axis=1).astype(jnp.bfloat16)
    route_hits = destination_slot[None, :, :] == jnp.arange(send_rows, dtype=jnp.int32)[:, None, None]
    slot_of_token = jnp.sum(route_hits.astype(jnp.int32), axis=2).astype(jnp.bfloat16)
    token_gradient = lax.dot_general(
        slot_of_token, came_back, (((0,), (0,)), ((), ())), preferred_element_type=jnp.float32
    ).astype(jnp.bfloat16)
    local_cotangent = local_cotangent_bf.astype(jnp.float32)
    hidden_totals = jnp.sum(local_cotangent[:, None, :] * out_rows, axis=2)
    gate_gradient = lax.psum(jnp.where(slot_alive_mask, hidden_totals, 0.0), "tensor")
    grad_gate_w, grad_up_w, grad_down_w = grads
    return (
        mixed,
        token_gradient,
        gate_gradient,
        grad_gate_w[None],
        grad_up_w[None],
        grad_down_w[None],
    )


def solution(mesh):
    in_specs = (
        P("expert", None),
        P("expert", None),
        P("expert", None),
        P("expert", None),
        P("expert", None),
        P("expert", None),
        P("expert", None, "tensor"),
        P("expert", None, "tensor"),
        P("expert", "tensor", None),
    )
    out_specs = (
        P("expert", "tensor"),
        P("expert", "tensor"),
        P("expert", None),
        P("expert", None, "tensor"),
        P("expert", None, "tensor"),
        P("expert", "tensor", None),
    )
    return jax.shard_map(local, mesh=mesh, in_specs=in_specs, out_specs=out_specs, check_vma=False)
```
